256 devices in a mesh: grp: 32 (over z, x), tp: 8 (over y, core).
Axes of the slice: x: 4, y: 4, z: 8, core: 2. Of those that a mesh axis runs over, the one named last changes fastest.
Arguments:
- tokens: bfloat16 [32768, 2048], P('grp'), may hold values from -6 to 6
- norm_gain: float32 [2048], replicated, may hold values from 0.5 to 7
- w_qkv: bfloat16 [2048, 3, 2048], P(None, None, 'tp'), may hold values from -0.125 to 0.125
- w_out: bfloat16 [2048, 2048], P('tp'), may hold values from -0.125 to 0.125
- a_in: bfloat16 [64, 2048, 48], P('grp', 'tp'), may hold values from -0.125 to 0.125
- b_in: bfloat16 [64, 3, 16, 2048], P('grp', None, None, 'tp'), may hold values from -1.5 to 1.5
- a_out: bfloat16 [64, 2048, 16], P('grp', 'tp'), may hold values from -0.125 to 0.125
- b_out: bfloat16 [64, 16, 2048], P('grp', None, 'tp'), may hold values from -1.5 to 1.5
- req_len: int32 [32, 4], replicated, may hold values from 1 to 512, 1024 in all within a row
- req_adapter: int32 [32, 4], replicated, may hold values from 0 to 63, as said below
- holder: int32 [64], replicated, may hold values from 0 to 63, each once
- page_table: int32 [32, 8], P('grp'), may hold values from 0 to 7, each once within a row
Outputs:
- layer_out: bfloat16 [32768, 2048], P('grp', 'tp')
- kv_pages: bfloat16 [256, 2, 128, 2048], P('grp', None, None, 'tp')
The draws below stay inside these ranges and needn't reach their ends.
Inputs may be any that keep to these rules, and one draw needn't show every extreme that they name: `req_adapter`: exactly 16 different adapters appear among all requests.
All inputs are finite; a program needn't handle non-finite values.
Results may differ from the reference program's by a relative error of at most 0.017.
The reference program's roundings to bfloat16 on the way count: a program that leaves them out, or rounds other values in their place, can miss the bound.
Values may be sent and summed in bfloat16 or wider, within the bound.
No kernel may reach another device: no remote copies, remote signals or barrier semaphores. Data moves between devices by JAX's collectives and lax.ppermute only.
A program may use at most 128 MiB of HBM per device.

```python
import math
import jax
import jax.numpy as jnp
import numpy as np
from jax import lax

D = 2048
HEADS = 16
HD = 128
R = 16
USED = 16
TOK_G = 1024
REQ = 4
PAGE = 128
MOST = 512
PAGES_G = 8
GROUPS = 32
ADAPTERS = 64
TOKENS = 32768
N_TP = 8


def draw_norm_gain(key, part):
    return jax.random.uniform(key, (D,), jnp.float32, 0.5, 1.5)


def draw_req_adapter(key, part):
    pick_key = jax.random.fold_in(key, 11)
    fill_key = jax.random.fold_in(key, 12)
    place_key = jax.random.fold_in(key, 13)
    chosen = jax.random.permutation(pick_key, ADAPTERS)[:USED]
    total_rows = GROUPS * REQ
    picked = jax.random.randint(fill_key, (total_rows,), 0, USED)
    places = jax.random.permutation(place_key, total_rows)[:USED]
    picked = picked.at[places].set(jnp.arange(USED, dtype=jnp.int32))
    return chosen[picked].astype(jnp.int32).reshape(GROUPS, REQ)


def block_scale(stream_key, shape, split, least, high):
    factor_of = 1.0
    for dim, shards_of in split:
        heights = jax.random.uniform(jax.random.fold_in(jax.random.fold_in(stream_key, 6), dim), (shards_of,), jnp.float32, least / len(split), high / len(split))
        factor_of = factor_of * jnp.repeat(jnp.exp(heights), shape[dim] // shards_of).reshape((-1,) + (1,) * (len(shape) - 1 - dim))
    return factor_of


def split_up(number_of, total, bound, skew):
    portions = [(1 << 20) // math.isqrt(grade ** skew) + 1 for grade in range(2, number_of + 1)]
    surplus, given = total - bound - (number_of - 1), [1] * (number_of - 1)
    while surplus > 0:
        free = [i for i in range(number_of - 1) if given[i] < bound]
        whole, budget = sum([portions[i] for i in free]), surplus
        for i in free:
            extra = min(bound - given[i], max(1, budget * portions[i] // whole), surplus)
            given[i] = given[i] + extra
            surplus = surplus - extra
    return np.array([bound] + given)


def ragged_sizes(rng, amount, total, bound, skew):
    if amount == 2:
        one = jax.random.randint(rng, (), max(1, total - bound), min(bound, total - 1) + 1)
        return jnp.stack([one, total - one])
    sizes = jnp.asarray(split_up(amount, total, bound, skew), jnp.int32)
    pairs = (amount - 1) // 2
    source_of, sink = sizes[1:1 + 2 * pairs:2], sizes[2:2 + 2 * pairs:2]
    slack = jnp.minimum(source_of - 1, bound - sink)
    shifted = jax.random.randint(jax.random.fold_in(rng, 1), (pairs,), 0, 1 << 20) % (slack + 1)
    sizes = sizes.at[1:1 + 2 * pairs:2].set(source_of - shifted).at[2:2 + 2 * pairs:2].set(sink + shifted)
    return sizes[jax.random.permutation(jax.random.fold_in(rng, 2), amount)]


def scatter_about(stream_key, shape, deviation, bound, split=(), kind=jnp.bfloat16):
    array = jax.random.normal(stream_key, shape, jnp.float32) * deviation
    if len(split) > 0:
        array = block_scale(stream_key, shape, split, -0.22, 0.18) * array
    return jnp.clip(array, min=-bound, max=bound).astype(kind)


def setup_inputs(seed: int = 0) -> dict:
    splits = jax.random.split(jax.random.key(seed), 13)
    tokens = scatter_about(splits[0], (TOKENS, D), 1.0, 6.0, ((0, 32),))
    norm_gain = draw_norm_gain(jax.random.fold_in(splits[12], 71), 0)
    w_qkv = scatter_about(splits[2], (D, 3, D), D ** -0.5, 0.125, ((2, 8),))
    w_out = scatter_about(splits[3], (D, D), D ** -0.5, 0.125, ((0, 8),))
    a_in = scatter_about(splits[4], (ADAPTERS, D, 3 * R), D ** -0.5, 0.125, ((0, 32), (1, 8)))
    b_in = scatter_about(splits[5], (ADAPTERS, 3, R, D), R ** -0.5, 1.5, ((0, 32), (3, 8)))
    a_out = scatter_about(splits[6], (ADAPTERS, D, R), D ** -0.5, 0.125, ((0, 32), (1, 8)))
    b_out = scatter_about(splits[7], (ADAPTERS, R, D), R ** -0.5, 1.5, ((0, 32), (2, 8)))
    req_len = jax.vmap(lambda own: ragged_sizes(own, REQ, TOK_G, MOST, 2))(jax.random.split(splits[8], GROUPS)).reshape((GROUPS, REQ)).astype(jnp.int32)
    req_adapter = draw_req_adapter(jax.random.fold_in(splits[12], 71), 0)
    holder = jax.random.permutation(splits[10], ADAPTERS).astype(jnp.int32)
    page_table = jax.vmap(lambda own: jax.random.permutation(own, PAGES_G))(jax.random.split(splits[11], GROUPS)).reshape((GROUPS, PAGES_G)).astype(jnp.int32)
    return dict(tokens=tokens, norm_gain=norm_gain, w_qkv=w_qkv, w_out=w_out, a_in=a_in, b_in=b_in, a_out=a_out, b_out=b_out, req_len=req_len, req_adapter=req_adapter, holder=holder, page_table=page_table)


EPSILON = 1e-05
THETA = 10000.0

def rms_norm(token_rows, norm_gain):
    values = token_rows.astype(jnp.float32)
    norm_scale = lax.rsqrt(lax.optimization_barrier(jnp.mean(values * values, axis=-1, keepdims=True)) + EPSILON)
    return (values * norm_scale * norm_gain).astype(jnp.bfloat16)

def request_layout(lengths, offset, tok_count):
    end_at = jnp.cumsum(lengths).astype(jnp.int32)
    starts = (end_at - lengths).astype(jnp.int32)
    row_ids = jnp.arange(tok_count, dtype=jnp.int32)
    segment = lax.optimization_barrier(jnp.sum((row_ids[:, None] >= end_at[None, :]).astype(jnp.int32), axis=1)).astype(jnp.int32)
    member = segment[:, None] == jnp.arange(lengths.shape[0], dtype=jnp.int32)[None, :]
    begin_at = lax.optimization_barrier(jnp.sum(jnp.where(member, starts[None, :], 0), axis=1)).astype(jnp.int32)
    position = (row_ids - begin_at + jnp.where(segment == 0, offset, 0)).astype(jnp.int32)
    return (segment, member, position)

def rotate(head_rows, position, head_dim):
    half_dim = head_dim // 2
    frequency = THETA ** (-(jnp.arange(half_dim, dtype=jnp.float32) * (2.0 / head_dim)))
    angles = position.astype(jnp.float32)[:, None] * frequency[None, :]
    cosine = jnp.cos(angles)[:, None, :]
    sine_part = jnp.sin(angles)[:, None, :]
    lower_half = head_rows[..., :half_dim]
    upper_half = head_rows[..., half_dim:]
    return jnp.concatenate([lower_half * cosine - upper_half * sine_part, upper_half * cosine + lower_half * sine_part], axis=-1)

def reference(tokens, norm_gain, w_qkv, w_out, a_in, b_in, a_out, b_out, req_len, req_adapter, holder, page_table):
    groups = req_len.shape[0]
    group_ids = jnp.arange(groups, dtype=jnp.int32)
    last_len = req_len[:, REQ - 1]
    previous_last = jnp.concatenate([jnp.zeros((1,), jnp.int32), last_len[:-1]]).astype(jnp.int32)
    continued = group_ids > 0
    offsets = jnp.where(continued, previous_last, 0).astype(jnp.int32)
    slots = holder[req_adapter]
    grouped = tokens.reshape(groups, TOK_G, D)
    w_flat = w_qkv.reshape(D, 3 * D)
    score_scale = 1.0 / math.sqrt(HD)

    def project(group_items):
        token_rows, lengths, slot_row, offset = group_items
        normed = rms_norm(token_rows, norm_gain)
        segment, member, position = request_layout(lengths, offset, TOK_G)
        member_f = member.astype(jnp.float32)
        down_f = jnp.einsum('td,rdk->trk', normed.astype(jnp.float32), a_in[slot_row].astype(jnp.float32))
        lowrank = lax.optimization_barrier(jnp.sum(down_f * member_f[:, :, None], axis=1)).astype(jnp.bfloat16)
        spread = (member_f[:, :, None] * lowrank.astype(jnp.float32)[:, None, :]).reshape(TOK_G, REQ, 3, R)
        delta_qkv = jnp.einsum('trck,rckd->tcd', spread, b_in[slot_row].astype(jnp.float32))
        base_qkv = jnp.dot(normed, w_flat, preferred_element_type=jnp.float32).reshape(TOK_G, 3, D)
        qkv = (base_qkv + delta_qkv).reshape(TOK_G, 3, HEADS, HD)
        query_rows = rotate(qkv[:, 0], position, HD).astype(jnp.bfloat16)
        key_rows = rotate(qkv[:, 1], position, HD).astype(jnp.bfloat16)
        value_rows = qkv[:, 2].astype(jnp.bfloat16)
        return (query_rows, key_rows, value_rows)
    queries, keys, values = lax.map(project, (grouped, req_len, slots, offsets))
    far_keys = jnp.concatenate([jnp.zeros_like(keys[:1]), keys[:-1]], axis=0)
    far_values = jnp.concatenate([jnp.zeros_like(values[:1]), values[:-1]], axis=0)

    def attend(group_items):
        query_rows, key_rows, value_rows, far_key, far_value, lengths, offset, flag_on, prev_len = group_items
        segment, member, position = request_layout(lengths, offset, TOK_G)
        row_ids = jnp.arange(TOK_G, dtype=jnp.int32)
        near_ok = (segment[:, None] == segment[None, :]) & (row_ids[None, :] <= row_ids[:, None])
        far_ok = flag_on & (segment[:, None] == 0) & (row_ids[None, :] >= TOK_G - prev_len)
        allowed = jnp.concatenate([far_ok, near_ok], axis=1)
        key_all = jnp.concatenate([far_key, key_rows], axis=0).astype(jnp.float32)
        value_all = jnp.concatenate([far_value, value_rows], axis=0).astype(jnp.float32)
        scores = jnp.einsum('thd,shd->hts', query_rows.astype(jnp.float32), key_all) * score_scale
        scores = jnp.where(allowed[None], scores, -jnp.inf)
        row_top = lax.optimization_barrier(jnp.max(scores, axis=-1, keepdims=True))
        weights = jnp.exp(scores - row_top)
        weights_bf = (weights / lax.optimization_barrier(jnp.sum(weights, axis=-1, keepdims=True))).astype(jnp.bfloat16)
        mixed_heads = jnp.einsum('hts,shd->thd', weights_bf.astype(jnp.float32), value_all)
        return mixed_heads.astype(jnp.bfloat16).reshape(TOK_G, D)
    attended = lax.map(attend, (queries, keys, values, far_keys, far_values, req_len, offsets, continued, previous_last))
    blocked_w = w_out.reshape(N_TP, D // N_TP, D).astype(jnp.float32)

    def finish(group_items):
        token_rows, attn_rows, lengths, slot_row = group_items
        segment, member, position = request_layout(lengths, jnp.int32(0), TOK_G)
        member_f = member.astype(jnp.float32)
        attn_f = attn_rows.astype(jnp.float32)
        pieces = jnp.einsum('tpd,pde->tpe', attn_f.reshape(TOK_G, N_TP, D // N_TP), blocked_w)
        pieces = lax.optimization_barrier(pieces.astype(jnp.bfloat16)).astype(jnp.float32)
        base_out = lax.optimization_barrier(jnp.sum(pieces, axis=1))
        down_o = jnp.einsum('td,rdk->trk', attn_f, a_out[slot_row].astype(jnp.float32))
        low_o = lax.optimization_barrier(jnp.sum(down_o * member_f[:, :, None], axis=1)).astype(jnp.bfloat16)
        spread_o = (member_f[:, :, None] * low_o.astype(jnp.float32)[:, None, :]).reshape(TOK_G, REQ * R)
        delta_o = jnp.dot(spread_o, b_out[slot_row].astype(jnp.float32).reshape(REQ * R, D))
        return (token_rows.astype(jnp.float32) + base_out + delta_o).astype(jnp.bfloat16)
    layer_out = lax.map(finish, (grouped, attended, req_len, slots)).reshape(groups * TOK_G, D)
    page_count = TOK_G // PAGE
    numbers = jnp.arange(page_count, dtype=jnp.int32)
    inverse = lax.optimization_barrier(jnp.sum(jnp.where(page_table[:, :, None] == numbers[None, None, :], numbers[None, :, None], 0), axis=1)).astype(jnp.int32)
    key_blocks = keys.reshape(groups, page_count, PAGE, D)
    value_blocks = values.reshape(groups, page_count, PAGE, D)
    both_blocks = jnp.stack([key_blocks, value_blocks], axis=2)

    def place_pages(block_set, page_order):
        return jnp.take(block_set, page_order, axis=0)
    kv_pages = jax.vmap(place_pages)(both_blocks, inverse).reshape(groups * page_count, 2, PAGE, D)
    return (layer_out, kv_pages)
```

```python
import math

import jax
import jax.numpy as jnp
from jax import lax
from jax.sharding import PartitionSpec as P

HD = 128
PAGE = 128


EPSILON = 1e-05
THETA = 10000.0


def shifted(block, axis, distance):
    devices = range(lax.axis_size(axis))
    route = [(i - distance, i) for i in devices if i - distance in devices]
    return lax.ppermute(block, axis, route)


USED = 16


def xor_allreduce(value, axis):
    count = lax.axis_size(axis)
    step = 1
    while step < count:
        route = [(i, i ^ step) for i in range(count)]
        value = value + lax.ppermute(value, axis, route)
        step *= 2
    return value


def fetch_adapters(stores, req_adapter, holder, wanted, group_id):
    held = stores[0].shape[0]
    total = holder.shape[0]
    names = jnp.arange(total, dtype=jnp.int32)
    used = jnp.any(req_adapter.reshape(-1)[:, None] == names[None, :], axis=0)
    rank = jnp.cumsum(used.astype(jnp.int32)) - 1
    picks = jnp.arange(USED, dtype=jnp.int32)
    hit = used[None, :] & (rank[None, :] == picks[:, None])
    chosen = jnp.sum(jnp.where(hit, names[None, :], 0), axis=1)
    slots = holder[chosen]
    mine = (slots // held) == group_id
    local_idx = slots % held
    flat = jnp.concatenate([s.reshape(held, -1) for s in stores], axis=1)
    compact = jnp.where(mine[:, None], jnp.take(flat, local_idx, axis=0), jnp.zeros((), flat.dtype))
    compact = lax.psum(compact, "grp")
    mine_rows = jnp.take(compact, rank[wanted], axis=0)
    out = []
    at = 0
    for s in stores:
        size = math.prod(s.shape[1:])
        out.append(mine_rows[:, at : at + size].reshape((wanted.shape[0],) + s.shape[1:]))
        at += size
    return tuple(out)


def rms_norm(token_rows, norm_gain):
    values = token_rows.astype(jnp.float32)
    norm_scale = lax.rsqrt(jnp.mean(values * values, axis=-1, keepdims=True) + EPSILON)
    return (values * norm_scale * norm_gain).astype(jnp.bfloat16)


def request_layout(lengths, offset, tok_count):
    end_at = jnp.cumsum(lengths)
    starts = end_at - lengths
    row_ids = jnp.arange(tok_count, dtype=jnp.int32)
    segment = jnp.sum((row_ids[:, None] >= end_at[None, :]).astype(jnp.int32), axis=1)
    member = segment[:, None] == jnp.arange(lengths.shape[0], dtype=jnp.int32)[None, :]
    begin_at = jnp.sum(jnp.where(member, starts[None, :], 0), axis=1)
    position = row_ids - begin_at + jnp.where(segment == 0, offset, 0)
    return (segment, member, position)


def rotate(head_rows, position, head_dim):
    half_dim = head_dim // 2
    frequency = THETA ** (-(jnp.arange(half_dim, dtype=jnp.float32) * (2.0 / head_dim)))
    angles = position.astype(jnp.float32)[:, None] * frequency[None, :]
    cosine = jnp.cos(angles)[:, None, :]
    sine_part = jnp.sin(angles)[:, None, :]
    lower_half = head_rows[..., :half_dim]
    upper_half = head_rows[..., half_dim:]
    return jnp.concatenate(
        [
            lower_half * cosine - upper_half * sine_part,
            upper_half * cosine + lower_half * sine_part,
        ],
        axis=-1,
    )


def local(
    tokens,
    norm_gain,
    w_qkv,
    w_out,
    a_in,
    b_in,
    a_out,
    b_out,
    req_len,
    req_adapter,
    holder,
    page_table,
):
    tok_count = tokens.shape[0]
    local_width = w_out.shape[0]
    local_heads = local_width // HD
    req_count = req_len.shape[1]
    rank_dim = a_out.shape[2]
    group_id = lax.axis_index("grp")
    tp_id = lax.axis_index("tp")
    lengths = lax.dynamic_index_in_dim(req_len, group_id, 0, keepdims=False)
    earlier = lax.dynamic_index_in_dim(req_len, jnp.maximum(group_id - 1, 0), 0, keepdims=False)
    continued = group_id > 0
    prev_len = earlier[req_count - 1]
    offset = jnp.where(continued, prev_len, 0)
    segment, member, position = request_layout(lengths, offset, tok_count)
    wanted = lax.dynamic_index_in_dim(req_adapter, group_id, 0, keepdims=False)
    sel_in, sel_up, sel_odown, sel_oup = fetch_adapters(
        (a_in, b_in, a_out, b_out), req_adapter, holder, wanted, group_id
    )
    member_f = member.astype(jnp.float32)
    pick_bf = member.astype(jnp.bfloat16)
    normed = rms_norm(tokens, norm_gain)
    own_cols = lax.dynamic_slice_in_dim(normed, tp_id * local_width, local_width, 1)
    down_f = jnp.einsum("td,rdk->trk", own_cols, sel_in, preferred_element_type=jnp.float32)
    lowrank_f = xor_allreduce(jnp.sum(down_f * member_f[:, :, None], axis=1), "tp")
    lowrank = lowrank_f.astype(jnp.bfloat16)
    spread = (pick_bf[:, :, None] * lowrank[:, None, :]).reshape(tok_count, req_count, 3, rank_dim)
    delta_qkv = jnp.einsum("trck,rckd->tcd", spread, sel_up, preferred_element_type=jnp.float32)
    base_qkv = jnp.dot(
        normed, w_qkv.reshape(w_qkv.shape[0], 3 * local_width), preferred_element_type=jnp.float32
    )
    qkv = (base_qkv.reshape(tok_count, 3, local_width) + delta_qkv).reshape(
        tok_count, 3, local_heads, HD
    )
    query_rows = rotate(qkv[:, 0], position, HD).astype(jnp.bfloat16)
    key_rows = rotate(qkv[:, 1], position, HD).astype(jnp.bfloat16).reshape(tok_count, local_width)
    value_rows = qkv[:, 2].astype(jnp.bfloat16).reshape(tok_count, local_width)
    row_ids = jnp.arange(tok_count, dtype=jnp.int32)
    far_key, far_value = shifted((key_rows, value_rows), "grp", 1)
    far_ok = continued & (segment[:, None] == 0) & (row_ids[None, :] >= tok_count - prev_len)
    far_count = far_key.shape[0]
    near_ok = (segment[:, None] == segment[None, :]) & (row_ids[None, :] <= row_ids[:, None])
    allowed = jnp.concatenate([far_ok, near_ok], axis=1)
    key_all = jnp.concatenate([far_key, key_rows], axis=0).reshape(
        far_count + tok_count, local_heads, HD
    )
    value_all = jnp.concatenate([far_value, value_rows], axis=0).reshape(
        far_count + tok_count, local_heads, HD
    )
    score_scale = 1.0 / math.sqrt(HD)
    scores = (
        jnp.einsum("thd,shd->hts", query_rows, key_all, preferred_element_type=jnp.float32)
        * score_scale
    )
    scores = jnp.where(allowed[None], scores, -jnp.inf)
    row_top = jnp.max(scores, axis=-1, keepdims=True)
    weights = jnp.exp(scores - row_top)
    weights_bf = (weights / jnp.sum(weights, axis=-1, keepdims=True)).astype(jnp.bfloat16)
    mixed_heads = jnp.einsum(
        "hts,shd->thd", weights_bf, value_all, preferred_element_type=jnp.float32
    )
    attended = mixed_heads.astype(jnp.bfloat16).reshape(tok_count, local_width)
    partial_value = jnp.dot(attended, w_out, preferred_element_type=jnp.float32)
    down_o = jnp.einsum("td,rdk->trk", attended, sel_odown, preferred_element_type=jnp.float32)
    low_part = jnp.sum(down_o * member_f[:, :, None], axis=1).astype(jnp.bfloat16)
    n_tp = lax.axis_size("tp")
    packed = jnp.concatenate(
        [
            partial_value.astype(jnp.bfloat16).reshape(tok_count, n_tp, local_width),
            jnp.broadcast_to(low_part[:, None, :], (tok_count, n_tp, rank_dim)),
        ],
        axis=2,
    ).reshape(tok_count, n_tp * (local_width + rank_dim))
    summed = lax.psum_scatter(packed, "tp", scatter_dimension=1, tiled=True)
    base_out = summed[:, :local_width].astype(jnp.float32)
    low_o = summed[:, local_width:]
    spread_o = (pick_bf[:, :, None] * low_o[:, None, :]).reshape(tok_count, req_count * rank_dim)
    delta_o = jnp.dot(
        spread_o,
        sel_oup.reshape(req_count * rank_dim, local_width),
        preferred_element_type=jnp.float32,
    )
    own_rows = lax.dynamic_slice_in_dim(tokens, tp_id * local_width, local_width, 1).astype(
        jnp.float32
    )
    layer_out = (own_rows + base_out + delta_o).astype(jnp.bfloat16)
    page_row = page_table[0]
    page_count = page_row.shape[0]
    numbers = jnp.arange(page_count, dtype=jnp.int32)
    inverse = jnp.sum(jnp.where(page_row[:, None] == numbers[None, :], numbers[:, None], 0), axis=0)
    both_blocks = jnp.stack(
        [
            key_rows.reshape(page_count, PAGE, local_width),
            value_rows.reshape(page_count, PAGE, local_width),
        ],
        axis=1,
    )
    kv_pages = jnp.take(both_blocks, inverse, axis=0)
    return (layer_out, kv_pages)


def solution(mesh):
    return jax.shard_map(
        local,
        mesh=mesh,
        in_specs=(
            P("grp", None),
            P(),
            P(None, None, "tp"),
            P("tp", None),
            P("grp", "tp", None),
            P("grp", None, None, "tp"),
            P("grp", "tp", None),
            P("grp", None, "tp"),
            P(),
            P(),
            P(),
            P("grp", None),
        ),
        out_specs=(P("grp", "tp"), P("grp", None, None, "tp")),
        check_vma=False,
    )
```

```python
import math

import jax
import jax.numpy as jnp
from jax import lax
from jax.sharding import PartitionSpec as P

HD = 128
PAGE = 128


EPSILON = 1e-05
THETA = 10000.0


def shifted(block, axis, distance):
    devices = range(lax.axis_size(axis))
    route = [(i - distance, i) for i in devices if i - distance in devices]
    return lax.ppermute(block, axis, route)


USED = 16


def xor_allreduce(value, axis):
    count = lax.axis_size(axis)
    step = 1
    while step < count:
        route = [(i, i ^ step) for i in range(count)]
        value = value + lax.ppermute(value, axis, route)
        step *= 2
    return value


def xor_halving_sum(buf, axis):
    count = lax.axis_size(axis)
    me = lax.axis_index(axis)
    rows = buf.shape[0]
    cur = buf.reshape((count, -1))
    dists = []
    step = 1
    while step < count:
        dists.append(step)
        step *= 2
    for d in dists:
        bit = (me // d) % 2
        cur = cur.reshape((2, -1) + cur.shape[1:])
        keep = lax.dynamic_index_in_dim(cur, bit, 0, keepdims=False)
        send = lax.dynamic_index_in_dim(cur, 1 - bit, 0, keepdims=False)
        cur = keep + lax.ppermute(send, axis, [(i, i ^ d) for i in range(count)])
    for d in reversed(dists):
        bit = (me // d) % 2
        other = lax.ppermute(cur, axis, [(i, i ^ d) for i in range(count)])
        cur = jnp.where(bit == 0, jnp.stack([cur, other]), jnp.stack([other, cur]))
    return cur.reshape(buf.shape)


def fetch_adapters(stores, req_adapter, holder, wanted, group_id):
    held = stores[0].shape[0]
    total = holder.shape[0]
    names = jnp.arange(total, dtype=jnp.int32)
    used = jnp.any(req_adapter.reshape(-1)[:, None] == names[None, :], axis=0)
    rank = jnp.cumsum(used.astype(jnp.int32)) - 1
    picks = jnp.arange(USED, dtype=jnp.int32)
    hit = used[None, :] & (rank[None, :] == picks[:, None])
    chosen = jnp.sum(jnp.where(hit, names[None, :], 0), axis=1)
    slots = holder[chosen]
    mine = (slots // held) == group_id
    local_idx = slots % held
    flat = jnp.concatenate([s.reshape(held, -1) for s in stores], axis=1)
    compact = jnp.where(mine[:, None], jnp.take(flat, local_idx, axis=0), jnp.zeros((), flat.dtype))
    compact = xor_halving_sum(compact, "grp")
    mine_rows = jnp.take(compact, rank[wanted], axis=0)
    out = []
    at = 0
    for s in stores:
        size = math.prod(s.shape[1:])
        out.append(mine_rows[:, at : at + size].reshape((wanted.shape[0],) + s.shape[1:]))
        at += size
    return tuple(out)


def rms_norm(token_rows, norm_gain):
    values = token_rows.astype(jnp.float32)
    norm_scale = lax.rsqrt(jnp.mean(values * values, axis=-1, keepdims=True) + EPSILON)
    return (values * norm_scale * norm_gain).astype(jnp.bfloat16)


def request_layout(lengths, offset, tok_count):
    end_at = jnp.cumsum(lengths)
    starts = end_at - lengths
    row_ids = jnp.arange(tok_count, dtype=jnp.int32)
    segment = jnp.sum((row_ids[:, None] >= end_at[None, :]).astype(jnp.int32), axis=1)
    member = segment[:, None] == jnp.arange(lengths.shape[0], dtype=jnp.int32)[None, :]
    begin_at = jnp.sum(jnp.where(member, starts[None, :], 0), axis=1)
    position = row_ids - begin_at + jnp.where(segment == 0, offset, 0)
    return (segment, member, position)


def rotate(head_rows, position, head_dim):
    half_dim = head_dim // 2
    frequency = THETA ** (-(jnp.arange(half_dim, dtype=jnp.float32) * (2.0 / head_dim)))
    angles = position.astype(jnp.float32)[:, None] * frequency[None, :]
    cosine = jnp.cos(angles)[:, None, :]
    sine_part = jnp.sin(angles)[:, None, :]
    lower_half = head_rows[..., :half_dim]
    upper_half = head_rows[..., half_dim:]
    return jnp.concatenate(
        [
            lower_half * cosine - upper_half * sine_part,
            upper_half * cosine + lower_half * sine_part,
        ],
        axis=-1,
    )


def local(
    tokens,
    norm_gain,
    w_qkv,
    w_out,
    a_in,
    b_in,
    a_out,
    b_out,
    req_len,
    req_adapter,
    holder,
    page_table,
):
    tok_count = tokens.shape[0]
    local_width = w_out.shape[0]
    local_heads = local_width // HD
    req_count = req_len.shape[1]
    rank_dim = a_out.shape[2]
    group_id = lax.axis_index("grp")
    tp_id = lax.axis_index("tp")
    lengths = lax.dynamic_index_in_dim(req_len, group_id, 0, keepdims=False)
    earlier = lax.dynamic_index_in_dim(req_len, jnp.maximum(group_id - 1, 0), 0, keepdims=False)
    continued = group_id > 0
    prev_len = earlier[req_count - 1]
    offset = jnp.where(continued, prev_len, 0)
    segment, member, position = request_layout(lengths, offset, tok_count)
    wanted = lax.dynamic_index_in_dim(req_adapter, group_id, 0, keepdims=False)
    sel_in, sel_up, sel_odown, sel_oup = fetch_adapters(
        (a_in, b_in, a_out, b_out), req_adapter, holder, wanted, group_id
    )
    member_f = member.astype(jnp.float32)
    pick_bf = member.astype(jnp.bfloat16)
    normed = rms_norm(tokens, norm_gain)
    own_cols = lax.dynamic_slice_in_dim(normed, tp_id * local_width, local_width, 1)
    down_f = jnp.einsum("td,rdk->trk", own_cols, sel_in, preferred_element_type=jnp.float32)
    lowrank_f = xor_allreduce(jnp.sum(down_f * member_f[:, :, None], axis=1), "tp")
    lowrank = lowrank_f.astype(jnp.bfloat16)
    spread = (pick_bf[:, :, None] * lowrank[:, None, :]).reshape(tok_count, req_count, 3, rank_dim)
    delta_qkv = jnp.einsum("trck,rckd->tcd", spread, sel_up, preferred_element_type=jnp.float32)
    base_qkv = jnp.dot(
        normed, w_qkv.reshape(w_qkv.shape[0], 3 * local_width), preferred_element_type=jnp.float32
    )
    qkv = (base_qkv.reshape(tok_count, 3, local_width) + delta_qkv).reshape(
        tok_count, 3, local_heads, HD
    )
    query_rows = rotate(qkv[:, 0], position, HD).astype(jnp.bfloat16)
    key_rows = rotate(qkv[:, 1], position, HD).astype(jnp.bfloat16).reshape(tok_count, local_width)
    value_rows = qkv[:, 2].astype(jnp.bfloat16).reshape(tok_count, local_width)
    row_ids = jnp.arange(tok_count, dtype=jnp.int32)
    far_key, far_value = shifted((key_rows, value_rows), "grp", 1)
    far_ok = continued & (segment[:, None] == 0) & (row_ids[None, :] >= tok_count - prev_len)
    far_count = far_key.shape[0]
    near_ok = (segment[:, None] == segment[None, :]) & (row_ids[None, :] <= row_ids[:, None])
    allowed = jnp.concatenate([far_ok, near_ok], axis=1)
    key_all = jnp.concatenate([far_key, key_rows], axis=0).reshape(
        far_count + tok_count, local_heads, HD
    )
    value_all = jnp.concatenate([far_value, value_rows], axis=0).reshape(
        far_count + tok_count, local_heads, HD
    )
    score_scale = 1.0 / math.sqrt(HD)
    scores = (
        jnp.einsum("thd,shd->hts", query_rows, key_all, preferred_element_type=jnp.float32)
        * score_scale
    )
    scores = jnp.where(allowed[None], scores, -jnp.inf)
    row_top = jnp.max(scores, axis=-1, keepdims=True)
    weights = jnp.exp(scores - row_top)
    weights_bf = (weights / jnp.sum(weights, axis=-1, keepdims=True)).astype(jnp.bfloat16)
    mixed_heads = jnp.einsum(
        "hts,shd->thd", weights_bf, value_all, preferred_element_type=jnp.float32
    )
    attended = mixed_heads.astype(jnp.bfloat16).reshape(tok_count, local_width)
    partial_value = jnp.dot(attended, w_out, preferred_element_type=jnp.float32)
    down_o = jnp.einsum("td,rdk->trk", attended, sel_odown, preferred_element_type=jnp.float32)
    low_part = jnp.sum(down_o * member_f[:, :, None], axis=1).astype(jnp.bfloat16)
    n_tp = lax.axis_size("tp")
    packed = jnp.concatenate(
        [
            partial_value.astype(jnp.bfloat16).reshape(tok_count, n_tp, local_width),
            jnp.broadcast_to(low_part[:, None, :], (tok_count, n_tp, rank_dim)),
        ],
        axis=2,
    ).reshape(tok_count, n_tp * (local_width + rank_dim))
    summed = lax.psum_scatter(packed, "tp", scatter_dimension=1, tiled=True)
    base_out = summed[:, :local_width].astype(jnp.float32)
    low_o = summed[:, local_width:]
    spread_o = (pick_bf[:, :, None] * low_o[:, None, :]).reshape(tok_count, req_count * rank_dim)
    delta_o = jnp.dot(
        spread_o,
        sel_oup.reshape(req_count * rank_dim, local_width),
        preferred_element_type=jnp.float32,
    )
    own_rows = lax.dynamic_slice_in_dim(tokens, tp_id * local_width, local_width, 1).astype(
        jnp.float32
    )
    layer_out = (own_rows + base_out + delta_o).astype(jnp.bfloat16)
    page_row = page_table[0]
    page_count = page_row.shape[0]
    numbers = jnp.arange(page_count, dtype=jnp.int32)
    inverse = jnp.sum(jnp.where(page_row[:, None] == numbers[None, :], numbers[:, None], 0), axis=0)
    both_blocks = jnp.stack(
        [
            key_rows.reshape(page_count, PAGE, local_width),
            value_rows.reshape(page_count, PAGE, local_width),
        ],
        axis=1,
    )
    kv_pages = jnp.take(both_blocks, inverse, axis=0)
    return (layer_out, kv_pages)


def solution(mesh):
    return jax.shard_map(
        local,
        mesh=mesh,
        in_specs=(
            P("grp", None),
            P(),
            P(None, None, "tp"),
            P("tp", None),
            P("grp", "tp", None),
            P("grp", None, None, "tp"),
            P("grp", "tp", None),
            P("grp", None, "tp"),
            P(),
            P(),
            P(),
            P("grp", None),
        ),
        out_specs=(P("grp", "tp"), P("grp", None, None, "tp")),
        check_vma=False,
    )
```

```python
import math

import jax
import jax.numpy as jnp
from jax import lax
from jax.sharding import PartitionSpec as P

HD = 128
PAGE = 128


EPSILON = 1e-05
THETA = 10000.0


def shifted(block, axis, distance):
    devices = range(lax.axis_size(axis))
    route = [(i - distance, i) for i in devices if i - distance in devices]
    return lax.ppermute(block, axis, route)


USED = 16


def xor_allreduce(value, axis):
    count = lax.axis_size(axis)
    step = 1
    while step < count:
        route = [(i, i ^ step) for i in range(count)]
        value = value + lax.ppermute(value, axis, route)
        step *= 2
    return value


def xor_halving_sum(buf, axis):
    count = lax.axis_size(axis)
    me = lax.axis_index(axis)
    rows = buf.shape[0]
    cur = buf.reshape((count, -1))
    dists = []
    step = 1
    while step < count:
        dists.append(step)
        step *= 2
    for d in dists:
        bit = (me // d) % 2
        cur = cur.reshape((2, -1) + cur.shape[1:])
        keep = lax.dynamic_index_in_dim(cur, bit, 0, keepdims=False)
        send = lax.dynamic_index_in_dim(cur, 1 - bit, 0, keepdims=False)
        cur = keep + lax.ppermute(send, axis, [(i, i ^ d) for i in range(count)])
    for d in reversed(dists):
        bit = (me // d) % 2
        other = lax.ppermute(cur, axis, [(i, i ^ d) for i in range(count)])
        cur = jnp.where(bit == 0, jnp.stack([cur, other]), jnp.stack([other, cur]))
    return cur.reshape(buf.shape)


def radix_sum(buf, axis, inner):
    count = lax.axis_size(axis)
    outer = count // inner
    me = lax.axis_index(axis)
    lo = me % inner
    hi = me // inner

    def route(shift, size, stride):
        pairs = []
        for i in range(count):
            pos = (i // stride) % size
            pairs.append((i, i + (((pos + shift) % size) - pos) * stride))
        return pairs

    def scatter_step(value, own, size, stride):
        pieces = value.reshape((size, -1))
        total = lax.dynamic_index_in_dim(pieces, own, 0, keepdims=False)
        for shift in range(1, size):
            part = lax.dynamic_index_in_dim(pieces, (own + shift) % size, 0, keepdims=False)
            total = total + lax.ppermute(part, axis, route(shift, size, stride))
        return total

    def gather_step(value, own, size, stride):
        got = [value]
        for shift in range(1, size):
            got.append(lax.ppermute(value, axis, route(shift, size, stride)))
        stack = jnp.stack(got)
        order = (own - jnp.arange(size, dtype=jnp.int32)) % size
        return jnp.take(stack, order, axis=0).reshape(-1)

    flat = buf.reshape(-1)
    part = scatter_step(flat, lo, inner, 1)
    part = scatter_step(part, hi, outer, inner)
    part = gather_step(part, hi, outer, inner)
    part = gather_step(part, lo, inner, 1)
    return part.reshape(buf.shape)


def fetch_adapters(stores, req_adapter, holder, wanted, group_id):
    held = stores[0].shape[0]
    total = holder.shape[0]
    names = jnp.arange(total, dtype=jnp.int32)
    used = jnp.any(req_adapter.reshape(-1)[:, None] == names[None, :], axis=0)
    rank = jnp.cumsum(used.astype(jnp.int32)) - 1
    picks = jnp.arange(USED, dtype=jnp.int32)
    hit = used[None, :] & (rank[None, :] == picks[:, None])
    chosen = jnp.sum(jnp.where(hit, names[None, :], 0), axis=1)
    slots = holder[chosen]
    mine = (slots // held) == group_id
    local_idx = slots % held
    flat = jnp.concatenate([s.reshape(held, -1) for s in stores], axis=1)
    compact = jnp.where(mine[:, None], jnp.take(flat, local_idx, axis=0), jnp.zeros((), flat.dtype))
    compact = radix_sum(compact, "grp", 4)
    mine_rows = jnp.take(compact, rank[wanted], axis=0)
    out = []
    at = 0
    for s in stores:
        size = math.prod(s.shape[1:])
        out.append(mine_rows[:, at : at + size].reshape((wanted.shape[0],) + s.shape[1:]))
        at += size
    return tuple(out)


def rms_norm(token_rows, norm_gain):
    values = token_rows.astype(jnp.float32)
    norm_scale = lax.rsqrt(jnp.mean(values * values, axis=-1, keepdims=True) + EPSILON)
    return (values * norm_scale * norm_gain).astype(jnp.bfloat16)


def request_layout(lengths, offset, tok_count):
    end_at = jnp.cumsum(lengths)
    starts = end_at - lengths
    row_ids = jnp.arange(tok_count, dtype=jnp.int32)
    segment = jnp.sum((row_ids[:, None] >= end_at[None, :]).astype(jnp.int32), axis=1)
    member = segment[:, None] == jnp.arange(lengths.shape[0], dtype=jnp.int32)[None, :]
    begin_at = jnp.sum(jnp.where(member, starts[None, :], 0), axis=1)
    position = row_ids - begin_at + jnp.where(segment == 0, offset, 0)
    return (segment, member, position)


def rotate(head_rows, position, head_dim):
    half_dim = head_dim // 2
    frequency = THETA ** (-(jnp.arange(half_dim, dtype=jnp.float32) * (2.0 / head_dim)))
    angles = position.astype(jnp.float32)[:, None] * frequency[None, :]
    cosine = jnp.cos(angles)[:, None, :]
    sine_part = jnp.sin(angles)[:, None, :]
    lower_half = head_rows[..., :half_dim]
    upper_half = head_rows[..., half_dim:]
    return jnp.concatenate(
        [
            lower_half * cosine - upper_half * sine_part,
            upper_half * cosine + lower_half * sine_part,
        ],
        axis=-1,
    )


def local(
    tokens,
    norm_gain,
    w_qkv,
    w_out,
    a_in,
    b_in,
    a_out,
    b_out,
    req_len,
    req_adapter,
    holder,
    page_table,
):
    tok_count = tokens.shape[0]
    local_width = w_out.shape[0]
    local_heads = local_width // HD
    req_count = req_len.shape[1]
    rank_dim = a_out.shape[2]
    group_id = lax.axis_index("grp")
    tp_id = lax.axis_index("tp")
    lengths = lax.dynamic_index_in_dim(req_len, group_id, 0, keepdims=False)
    earlier = lax.dynamic_index_in_dim(req_len, jnp.maximum(group_id - 1, 0), 0, keepdims=False)
    continued = group_id > 0
    prev_len = earlier[req_count - 1]
    offset = jnp.where(continued, prev_len, 0)
    segment, member, position = request_layout(lengths, offset, tok_count)
    wanted = lax.dynamic_index_in_dim(req_adapter, group_id, 0, keepdims=False)
    sel_in, sel_up, sel_odown, sel_oup = fetch_adapters(
        (a_in, b_in, a_out, b_out), req_adapter, holder, wanted, group_id
    )
    member_f = member.astype(jnp.float32)
    pick_bf = member.astype(jnp.bfloat16)
    normed = rms_norm(tokens, norm_gain)
    own_cols = lax.dynamic_slice_in_dim(normed, tp_id * local_width, local_width, 1)
    down_f = jnp.einsum("td,rdk->trk", own_cols, sel_in, preferred_element_type=jnp.float32)
    lowrank_f = xor_allreduce(jnp.sum(down_f * member_f[:, :, None], axis=1), "tp")
    lowrank = lowrank_f.astype(jnp.bfloat16)
    spread = (pick_bf[:, :, None] * lowrank[:, None, :]).reshape(tok_count, req_count, 3, rank_dim)
    delta_qkv = jnp.einsum("trck,rckd->tcd", spread, sel_up, preferred_element_type=jnp.float32)
    base_qkv = jnp.dot(
        normed, w_qkv.reshape(w_qkv.shape[0], 3 * local_width), preferred_element_type=jnp.float32
    )
    qkv = (base_qkv.reshape(tok_count, 3, local_width) + delta_qkv).reshape(
        tok_count, 3, local_heads, HD
    )
    query_rows = rotate(qkv[:, 0], position, HD).astype(jnp.bfloat16)
    key_rows = rotate(qkv[:, 1], position, HD).astype(jnp.bfloat16).reshape(tok_count, local_width)
    value_rows = qkv[:, 2].astype(jnp.bfloat16).reshape(tok_count, local_width)
    row_ids = jnp.arange(tok_count, dtype=jnp.int32)
    far_key, far_value = shifted((key_rows, value_rows), "grp", 1)
    far_ok = continued & (segment[:, None] == 0) & (row_ids[None, :] >= tok_count - prev_len)
    far_count = far_key.shape[0]
    near_ok = (segment[:, None] == segment[None, :]) & (row_ids[None, :] <= row_ids[:, None])
    allowed = jnp.concatenate([far_ok, near_ok], axis=1)
    key_all = jnp.concatenate([far_key, key_rows], axis=0).reshape(
        far_count + tok_count, local_heads, HD
    )
    value_all = jnp.concatenate([far_value, value_rows], axis=0).reshape(
        far_count + tok_count, local_heads, HD
    )
    score_scale = 1.0 / math.sqrt(HD)
    scores = (
        jnp.einsum("thd,shd->hts", query_rows, key_all, preferred_element_type=jnp.float32)
        * score_scale
    )
    scores = jnp.where(allowed[None], scores, -jnp.inf)
    row_top = jnp.max(scores, axis=-1, keepdims=True)
    weights = jnp.exp(scores - row_top)
    weights_bf = (weights / jnp.sum(weights, axis=-1, keepdims=True)).astype(jnp.bfloat16)
    mixed_heads = jnp.einsum(
        "hts,shd->thd", weights_bf, value_all, preferred_element_type=jnp.float32
    )
    attended = mixed_heads.astype(jnp.bfloat16).reshape(tok_count, local_width)
    partial_value = jnp.dot(attended, w_out, preferred_element_type=jnp.float32)
    down_o = jnp.einsum("td,rdk->trk", attended, sel_odown, preferred_element_type=jnp.float32)
    low_part = jnp.sum(down_o * member_f[:, :, None], axis=1).astype(jnp.bfloat16)
    low_o = xor_allreduce(low_part, "tp")
    base_out = lax.psum_scatter(
        partial_value.astype(jnp.bfloat16), "tp", scatter_dimension=1, tiled=True
    ).astype(jnp.float32)
    spread_o = (pick_bf[:, :, None] * low_o[:, None, :]).reshape(tok_count, req_count * rank_dim)
    delta_o = jnp.dot(
        spread_o,
        sel_oup.reshape(req_count * rank_dim, local_width),
        preferred_element_type=jnp.float32,
    )
    own_rows = lax.dynamic_slice_in_dim(tokens, tp_id * local_width, local_width, 1).astype(
        jnp.float32
    )
    layer_out = (own_rows + base_out + delta_o).astype(jnp.bfloat16)
    page_row = page_table[0]
    page_count = page_row.shape[0]
    numbers = jnp.arange(page_count, dtype=jnp.int32)
    inverse = jnp.sum(jnp.where(page_row[:, None] == numbers[None, :], numbers[:, None], 0), axis=0)
    both_blocks = jnp.stack(
        [
            key_rows.reshape(page_count, PAGE, local_width),
            value_rows.reshape(page_count, PAGE, local_width),
        ],
        axis=1,
    )
    kv_pages = jnp.take(both_blocks, inverse, axis=0)
    return (layer_out, kv_pages)


def solution(mesh):
    return jax.shard_map(
        local,
        mesh=mesh,
        in_specs=(
            P("grp", None),
            P(),
            P(None, None, "tp"),
            P("tp", None),
            P("grp", "tp", None),
            P("grp", None, None, "tp"),
            P("grp", "tp", None),
            P("grp", None, "tp"),
            P(),
            P(),
            P(),
            P("grp", None),
        ),
        out_specs=(P("grp", "tp"), P("grp", None, None, "tp")),
        check_vma=False,
    )
```

```python
import math

import jax
import jax.numpy as jnp
from jax import lax
from jax.sharding import PartitionSpec as P

HD = 128
PAGE = 128


EPSILON = 1e-05
THETA = 10000.0


def shifted(block, axis, distance):
    devices = range(lax.axis_size(axis))
    route = [(i - distance, i) for i in devices if i - distance in devices]
    return lax.ppermute(block, axis, route)


USED = 16


def xor_allreduce(value, axis):
    count = lax.axis_size(axis)
    step = 1
    while step < count:
        route = [(i, i ^ step) for i in range(count)]
        value = value + lax.ppermute(value, axis, route)
        step *= 2
    return value


def xor_halving_sum(buf, axis):
    count = lax.axis_size(axis)
    me = lax.axis_index(axis)
    rows = buf.shape[0]
    cur = buf.reshape((count, -1))
    dists = []
    step = 1
    while step < count:
        dists.append(step)
        step *= 2
    for d in dists:
        bit = (me // d) % 2
        cur = cur.reshape((2, -1) + cur.shape[1:])
        keep = lax.dynamic_index_in_dim(cur, bit, 0, keepdims=False)
        send = lax.dynamic_index_in_dim(cur, 1 - bit, 0, keepdims=False)
        cur = keep + lax.ppermute(send, axis, [(i, i ^ d) for i in range(count)])
    for d in reversed(dists):
        bit = (me // d) % 2
        other = lax.ppermute(cur, axis, [(i, i ^ d) for i in range(count)])
        cur = jnp.where(bit == 0, jnp.stack([cur, other]), jnp.stack([other, cur]))
    return cur.reshape(buf.shape)


def radix_sum(buf, axis, inner):
    count = lax.axis_size(axis)
    outer = count // inner
    me = lax.axis_index(axis)
    lo = me % inner
    hi = me // inner

    def route(shift, size, stride):
        pairs = []
        for i in range(count):
            pos = (i // stride) % size
            pairs.append((i, i + (((pos + shift) % size) - pos) * stride))
        return pairs

    def scatter_step(value, own, size, stride):
        pieces = value.reshape((size, -1))
        total = lax.dynamic_index_in_dim(pieces, own, 0, keepdims=False)
        for shift in range(1, size):
            part = lax.dynamic_index_in_dim(pieces, (own + shift) % size, 0, keepdims=False)
            total = total + lax.ppermute(part, axis, route(shift, size, stride))
        return total

    def gather_step(value, own, size, stride):
        got = [value]
        for shift in range(1, size):
            got.append(lax.ppermute(value, axis, route(shift, size, stride)))
        stack = jnp.stack(got)
        order = (own - jnp.arange(size, dtype=jnp.int32)) % size
        return jnp.take(stack, order, axis=0).reshape(-1)

    flat = buf.reshape(-1)
    part = scatter_step(flat, lo, inner, 1)
    step = inner
    while step < count:
        part = part + lax.ppermute(part, axis, [(i, i ^ step) for i in range(count)])
        step *= 2
    part = gather_step(part, lo, inner, 1)
    return part.reshape(buf.shape)


def fetch_adapters(stores, req_adapter, holder, wanted, group_id):
    held = stores[0].shape[0]
    total = holder.shape[0]
    names = jnp.arange(total, dtype=jnp.int32)
    used = jnp.any(req_adapter.reshape(-1)[:, None] == names[None, :], axis=0)
    rank = jnp.cumsum(used.astype(jnp.int32)) - 1
    picks = jnp.arange(USED, dtype=jnp.int32)
    hit = used[None, :] & (rank[None, :] == picks[:, None])
    chosen = jnp.sum(jnp.where(hit, names[None, :], 0), axis=1)
    slots = holder[chosen]
    mine = (slots // held) == group_id
    local_idx = slots % held
    flat = jnp.concatenate([s.reshape(held, -1) for s in stores], axis=1)
    pick = mine[:, None] & (local_idx[:, None] == jnp.arange(held, dtype=jnp.int32)[None, :])
    compact = jnp.sum(jnp.where(pick[:, :, None], flat[None], jnp.zeros((), flat.dtype)), axis=1)
    compact = radix_sum(compact, "grp", 4)
    mine_rows = jnp.take(compact, rank[wanted], axis=0)
    out = []
    at = 0
    for s in stores:
        size = math.prod(s.shape[1:])
        out.append(mine_rows[:, at : at + size].reshape((wanted.shape[0],) + s.shape[1:]))
        at += size
    return tuple(out)


def rms_norm(token_rows, norm_gain):
    values = token_rows.astype(jnp.float32)
    norm_scale = lax.rsqrt(jnp.mean(values * values, axis=-1, keepdims=True) + EPSILON)
    return (values * norm_scale * norm_gain).astype(jnp.bfloat16)


def request_layout(lengths, offset, tok_count):
    end_at = jnp.cumsum(lengths)
    starts = end_at - lengths
    row_ids = jnp.arange(tok_count, dtype=jnp.int32)
    segment = jnp.sum((row_ids[:, None] >= end_at[None, :]).astype(jnp.int32), axis=1)
    member = segment[:, None] == jnp.arange(lengths.shape[0], dtype=jnp.int32)[None, :]
    begin_at = jnp.sum(jnp.where(member, starts[None, :], 0), axis=1)
    position = row_ids - begin_at + jnp.where(segment == 0, offset, 0)
    return (segment, member, position)


def rotate(head_rows, position, head_dim):
    half_dim = head_dim // 2
    frequency = THETA ** (-(jnp.arange(half_dim, dtype=jnp.float32) * (2.0 / head_dim)))
    angles = position.astype(jnp.float32)[:, None] * frequency[None, :]
    cosine = jnp.cos(angles)[:, None, :]
    sine_part = jnp.sin(angles)[:, None, :]
    lower_half = head_rows[..., :half_dim]
    upper_half = head_rows[..., half_dim:]
    return jnp.concatenate(
        [
            lower_half * cosine - upper_half * sine_part,
            upper_half * cosine + lower_half * sine_part,
        ],
        axis=-1,
    )


def local(
    tokens,
    norm_gain,
    w_qkv,
    w_out,
    a_in,
    b_in,
    a_out,
    b_out,
    req_len,
    req_adapter,
    holder,
    page_table,
):
    tok_count = tokens.shape[0]
    local_width = w_out.shape[0]
    local_heads = local_width // HD
    req_count = req_len.shape[1]
    rank_dim = a_out.shape[2]
    group_id = lax.axis_index("grp")
    tp_id = lax.axis_index("tp")
    lengths = lax.dynamic_index_in_dim(req_len, group_id, 0, keepdims=False)
    earlier = lax.dynamic_index_in_dim(req_len, jnp.maximum(group_id - 1, 0), 0, keepdims=False)
    continued = group_id > 0
    prev_len = earlier[req_count - 1]
    offset = jnp.where(continued, prev_len, 0)
    segment, member, position = request_layout(lengths, offset, tok_count)
    wanted = lax.dynamic_index_in_dim(req_adapter, group_id, 0, keepdims=False)
    sel_in, sel_up, sel_odown, sel_oup = fetch_adapters(
        (a_in, b_in, a_out, b_out), req_adapter, holder, wanted, group_id
    )
    member_f = member.astype(jnp.float32)
    pick_bf = member.astype(jnp.bfloat16)
    normed = rms_norm(tokens, norm_gain)
    own_cols = lax.dynamic_slice_in_dim(normed, tp_id * local_width, local_width, 1)
    down_f = jnp.einsum("td,rdk->trk", own_cols, sel_in, preferred_element_type=jnp.float32)
    lowrank_f = xor_allreduce(jnp.sum(down_f * member_f[:, :, None], axis=1), "tp")
    lowrank = lowrank_f.astype(jnp.bfloat16)
    spread = (pick_bf[:, :, None] * lowrank[:, None, :]).reshape(tok_count, req_count, 3, rank_dim)
    delta_qkv = jnp.einsum("trck,rckd->tcd", spread, sel_up, preferred_element_type=jnp.float32)
    base_qkv = jnp.dot(
        normed, w_qkv.reshape(w_qkv.shape[0], 3 * local_width), preferred_element_type=jnp.float32
    )
    qkv = (base_qkv.reshape(tok_count, 3, local_width) + delta_qkv).reshape(
        tok_count, 3, local_heads, HD
    )
    query_rows = rotate(qkv[:, 0], position, HD).astype(jnp.bfloat16)
    key_rows = rotate(qkv[:, 1], position, HD).astype(jnp.bfloat16).reshape(tok_count, local_width)
    value_rows = qkv[:, 2].astype(jnp.bfloat16).reshape(tok_count, local_width)
    row_ids = jnp.arange(tok_count, dtype=jnp.int32)
    far_key, far_value = shifted((key_rows, value_rows), "grp", 1)
    far_ok = continued & (segment[:, None] == 0) & (row_ids[None, :] >= tok_count - prev_len)
    far_count = far_key.shape[0]
    near_ok = (segment[:, None] == segment[None, :]) & (row_ids[None, :] <= row_ids[:, None])
    allowed = jnp.concatenate([far_ok, near_ok], axis=1)
    value_all = jnp.concatenate([far_value, value_rows], axis=0).reshape(
        far_count + tok_count, local_heads, HD
    )
    score_scale = 1.0 / math.sqrt(HD)
    near_scores = jnp.einsum(
        "thd,shd->hts",
        query_rows,
        key_rows.reshape(tok_count, local_heads, HD),
        preferred_element_type=jnp.float32,
    )
    far_scores = jnp.einsum(
        "thd,shd->hts",
        query_rows,
        far_key.reshape(far_count, local_heads, HD),
        preferred_element_type=jnp.float32,
    )
    scores = jnp.concatenate([far_scores, near_scores], axis=-1) * score_scale
    scores = jnp.where(allowed[None], scores, -jnp.inf)
    row_top = jnp.max(scores, axis=-1, keepdims=True)
    weights = jnp.exp(scores - row_top)
    weights_bf = (weights / jnp.sum(weights, axis=-1, keepdims=True)).astype(jnp.bfloat16)
    mixed_heads = jnp.einsum(
        "hts,shd->thd", weights_bf, value_all, preferred_element_type=jnp.float32
    )
    attended = mixed_heads.astype(jnp.bfloat16).reshape(tok_count, local_width)
    partial_value = jnp.dot(attended, w_out, preferred_element_type=jnp.float32)
    down_o = jnp.einsum("td,rdk->trk", attended, sel_odown, preferred_element_type=jnp.float32)
    low_part = jnp.sum(down_o * member_f[:, :, None], axis=1).astype(jnp.bfloat16)
    low_o = xor_allreduce(low_part, "tp")
    base_out = lax.psum_scatter(
        partial_value.astype(jnp.bfloat16), "tp", scatter_dimension=1, tiled=True
    ).astype(jnp.float32)
    spread_o = (pick_bf[:, :, None] * low_o[:, None, :]).reshape(tok_count, req_count * rank_dim)
    delta_o = jnp.dot(
        spread_o,
        sel_oup.reshape(req_count * rank_dim, local_width),
        preferred_element_type=jnp.float32,
    )
    own_rows = lax.dynamic_slice_in_dim(tokens, tp_id * local_width, local_width, 1).astype(
        jnp.float32
    )
    layer_out = (own_rows + base_out + delta_o).astype(jnp.bfloat16)
    page_row = page_table[0]
    page_count = page_row.shape[0]
    numbers = jnp.arange(page_count, dtype=jnp.int32)
    inverse = jnp.sum(jnp.where(page_row[:, None] == numbers[None, :], numbers[:, None], 0), axis=0)
    both_blocks = jnp.stack(
        [
            key_rows.reshape(page_count, PAGE, local_width),
            value_rows.reshape(page_count, PAGE, local_width),
        ],
        axis=1,
    )
    kv_pages = jnp.take(both_blocks, inverse, axis=0)
    return (layer_out, kv_pages)


def solution(mesh):
    return jax.shard_map(
        local,
        mesh=mesh,
        in_specs=(
            P("grp", None),
            P(),
            P(None, None, "tp"),
            P("tp", None),
            P("grp", "tp", None),
            P("grp", None, None, "tp"),
            P("grp", "tp", None),
            P("grp", None, "tp"),
            P(),
            P(),
            P(),
            P("grp", None),
        ),
        out_specs=(P("grp", "tp"), P("grp", None, None, "tp")),
        check_vma=False,
    )
```

```python
import math

import jax
import jax.numpy as jnp
from jax import lax
from jax.sharding import PartitionSpec as P

HD = 128
PAGE = 128


EPSILON = 1e-05
THETA = 10000.0


def shifted(block, axis, distance):
    devices = range(lax.axis_size(axis))
    route = [(i - distance, i) for i in devices if i - distance in devices]
    return lax.ppermute(block, axis, route)


USED = 16


def xor_allreduce(value, axis):
    count = lax.axis_size(axis)
    step = 1
    while step < count:
        route = [(i, i ^ step) for i in range(count)]
        value = value + lax.ppermute(value, axis, route)
        step *= 2
    return value


def xor_halving_sum(buf, axis):
    count = lax.axis_size(axis)
    me = lax.axis_index(axis)
    rows = buf.shape[0]
    cur = buf.reshape((count, -1))
    dists = []
    step = 1
    while step < count:
        dists.append(step)
        step *= 2
    for d in dists:
        bit = (me // d) % 2
        cur = cur.reshape((2, -1) + cur.shape[1:])
        keep = lax.dynamic_index_in_dim(cur, bit, 0, keepdims=False)
        send = lax.dynamic_index_in_dim(cur, 1 - bit, 0, keepdims=False)
        cur = keep + lax.ppermute(send, axis, [(i, i ^ d) for i in range(count)])
    for d in reversed(dists):
        bit = (me // d) % 2
        other = lax.ppermute(cur, axis, [(i, i ^ d) for i in range(count)])
        cur = jnp.where(bit == 0, jnp.stack([cur, other]), jnp.stack([other, cur]))
    return cur.reshape(buf.shape)


def radix_sum(buf, axis, inner):
    count = lax.axis_size(axis)
    outer = count // inner
    me = lax.axis_index(axis)
    lo = me % inner
    hi = me // inner

    def route(shift, size, stride):
        pairs = []
        for i in range(count):
            pos = (i // stride) % size
            pairs.append((i, i + (((pos + shift) % size) - pos) * stride))
        return pairs

    def scatter_step(value, own, size, stride):
        pieces = value.reshape((size, -1))
        total = lax.dynamic_index_in_dim(pieces, own, 0, keepdims=False)
        for shift in range(1, size):
            part = lax.dynamic_index_in_dim(pieces, (own + shift) % size, 0, keepdims=False)
            total = total + lax.ppermute(part, axis, route(shift, size, stride))
        return total

    def gather_step(value, own, size, stride):
        got = [value]
        for shift in range(1, size):
            got.append(lax.ppermute(value, axis, route(shift, size, stride)))
        stack = jnp.stack(got)
        order = (own - jnp.arange(size, dtype=jnp.int32)) % size
        return jnp.take(stack, order, axis=0).reshape(-1)

    flat = buf.reshape(-1)
    part = scatter_step(flat, lo, inner, 1)
    step = inner
    while step < count:
        part = part + lax.ppermute(part, axis, [(i, i ^ step) for i in range(count)])
        step *= 2
    part = gather_step(part, lo, inner, 1)
    return part.reshape(buf.shape)


def tp_reduce_scatter(partial, low, axis):
    count = lax.axis_size(axis)
    me = lax.axis_index(axis)
    core = me % 2
    chip = me // 2
    chips = count // 2
    tok, width = partial.shape
    part_w = width // count
    blocks = partial.astype(jnp.bfloat16).reshape(tok, chips, 2, part_w)
    low_rep = jnp.broadcast_to(low.astype(jnp.bfloat16)[:, None, :], (tok, chips, low.shape[1]))
    own = lax.dynamic_index_in_dim(blocks, core, 2, keepdims=False)
    away = lax.dynamic_index_in_dim(blocks, 1 - core, 2, keepdims=False)
    msg = jnp.concatenate([away, low_rep], axis=2)
    got = lax.ppermute(msg, axis, [(i, i ^ 1) for i in range(count)])
    chip_sum = jnp.concatenate([own, low_rep], axis=2).astype(jnp.float32) + got.astype(jnp.float32)
    total = lax.dynamic_index_in_dim(chip_sum, chip, 1, keepdims=False)
    for shift in range(1, chips):
        piece = lax.dynamic_index_in_dim(chip_sum, (chip + shift) % chips, 1, keepdims=False)
        route = [(i, ((i // 2 + shift) % chips) * 2 + i % 2) for i in range(count)]
        total = total + lax.ppermute(piece.astype(jnp.bfloat16), axis, route).astype(jnp.float32)
    return total[:, :part_w], total[:, part_w:]


def fetch_adapters(stores, req_adapter, holder, wanted, group_id):
    held = stores[0].shape[0]
    total = holder.shape[0]
    names = jnp.arange(total, dtype=jnp.int32)
    used = jnp.any(req_adapter.reshape(-1)[:, None] == names[None, :], axis=0)
    rank = jnp.cumsum(used.astype(jnp.int32)) - 1
    picks = jnp.arange(USED, dtype=jnp.int32)
    hit = used[None, :] & (rank[None, :] == picks[:, None])
    chosen = jnp.sum(jnp.where(hit, names[None, :], 0), axis=1)
    slots = holder[chosen]
    mine = (slots // held) == group_id
    local_idx = slots % held
    flat = jnp.concatenate([s.reshape(held, -1) for s in stores], axis=1)
    pick = mine[:, None] & (local_idx[:, None] == jnp.arange(held, dtype=jnp.int32)[None, :])
    compact = jnp.sum(jnp.where(pick[:, :, None], flat[None], jnp.zeros((), flat.dtype)), axis=1)
    compact = radix_sum(compact, "grp", 4)
    mine_rows = jnp.take(compact, rank[wanted], axis=0)
    out = []
    at = 0
    for s in stores:
        size = math.prod(s.shape[1:])
        out.append(mine_rows[:, at : at + size].reshape((wanted.shape[0],) + s.shape[1:]))
        at += size
    return tuple(out)


def rms_norm(token_rows, norm_gain):
    values = token_rows.astype(jnp.float32)
    norm_scale = lax.rsqrt(jnp.mean(values * values, axis=-1, keepdims=True) + EPSILON)
    return (values * norm_scale * norm_gain).astype(jnp.bfloat16)


def request_layout(lengths, offset, tok_count):
    end_at = jnp.cumsum(lengths)
    starts = end_at - lengths
    row_ids = jnp.arange(tok_count, dtype=jnp.int32)
    segment = jnp.sum((row_ids[:, None] >= end_at[None, :]).astype(jnp.int32), axis=1)
    member = segment[:, None] == jnp.arange(lengths.shape[0], dtype=jnp.int32)[None, :]
    begin_at = jnp.sum(jnp.where(member, starts[None, :], 0), axis=1)
    position = row_ids - begin_at + jnp.where(segment == 0, offset, 0)
    return (segment, member, position)


def rotate(head_rows, position, head_dim):
    half_dim = head_dim // 2
    frequency = THETA ** (-(jnp.arange(half_dim, dtype=jnp.float32) * (2.0 / head_dim)))
    angles = position.astype(jnp.float32)[:, None] * frequency[None, :]
    cosine = jnp.cos(angles)[:, None, :]
    sine_part = jnp.sin(angles)[:, None, :]
    lower_half = head_rows[..., :half_dim]
    upper_half = head_rows[..., half_dim:]
    return jnp.concatenate(
        [
            lower_half * cosine - upper_half * sine_part,
            upper_half * cosine + lower_half * sine_part,
        ],
        axis=-1,
    )


def local(
    tokens,
    norm_gain,
    w_qkv,
    w_out,
    a_in,
    b_in,
    a_out,
    b_out,
    req_len,
    req_adapter,
    holder,
    page_table,
):
    tok_count = tokens.shape[0]
    local_width = w_out.shape[0]
    local_heads = local_width // HD
    req_count = req_len.shape[1]
    rank_dim = a_out.shape[2]
    group_id = lax.axis_index("grp")
    tp_id = lax.axis_index("tp")
    lengths = lax.dynamic_index_in_dim(req_len, group_id, 0, keepdims=False)
    earlier = lax.dynamic_index_in_dim(req_len, jnp.maximum(group_id - 1, 0), 0, keepdims=False)
    continued = group_id > 0
    prev_len = earlier[req_count - 1]
    offset = jnp.where(continued, prev_len, 0)
    segment, member, position = request_layout(lengths, offset, tok_count)
    wanted = lax.dynamic_index_in_dim(req_adapter, group_id, 0, keepdims=False)
    sel_in, sel_up, sel_odown, sel_oup = fetch_adapters(
        (a_in, b_in, a_out, b_out), req_adapter, holder, wanted, group_id
    )
    member_f = member.astype(jnp.float32)
    pick_bf = member.astype(jnp.bfloat16)
    normed = rms_norm(tokens, norm_gain)
    own_cols = lax.dynamic_slice_in_dim(normed, tp_id * local_width, local_width, 1)
    down_f = jnp.einsum("td,rdk->trk", own_cols, sel_in, preferred_element_type=jnp.float32)
    lowrank_f = xor_allreduce(jnp.sum(down_f * member_f[:, :, None], axis=1), "tp")
    lowrank = lowrank_f.astype(jnp.bfloat16)
    spread = (pick_bf[:, :, None] * lowrank[:, None, :]).reshape(tok_count, req_count, 3, rank_dim)
    delta_qkv = jnp.einsum("trck,rckd->tcd", spread, sel_up, preferred_element_type=jnp.float32)
    base_qkv = jnp.dot(
        normed, w_qkv.reshape(w_qkv.shape[0], 3 * local_width), preferred_element_type=jnp.float32
    )
    qkv = (base_qkv.reshape(tok_count, 3, local_width) + delta_qkv).reshape(
        tok_count, 3, local_heads, HD
    )
    query_rows = rotate(qkv[:, 0], position, HD).astype(jnp.bfloat16)
    key_rows = rotate(qkv[:, 1], position, HD).astype(jnp.bfloat16).reshape(tok_count, local_width)
    value_rows = qkv[:, 2].astype(jnp.bfloat16).reshape(tok_count, local_width)
    row_ids = jnp.arange(tok_count, dtype=jnp.int32)
    far_key, far_value = shifted((key_rows, value_rows), "grp", 1)
    far_ok = continued & (segment[:, None] == 0) & (row_ids[None, :] >= tok_count - prev_len)
    far_count = far_key.shape[0]
    near_ok = (segment[:, None] == segment[None, :]) & (row_ids[None, :] <= row_ids[:, None])
    allowed = jnp.concatenate([far_ok, near_ok], axis=1)
    value_all = jnp.concatenate([far_value, value_rows], axis=0).reshape(
        far_count + tok_count, local_heads, HD
    )
    score_scale = 1.0 / math.sqrt(HD)
    near_scores = jnp.einsum(
        "thd,shd->hts",
        query_rows,
        key_rows.reshape(tok_count, local_heads, HD),
        preferred_element_type=jnp.float32,
    )
    far_scores = jnp.einsum(
        "thd,shd->hts",
        query_rows,
        far_key.reshape(far_count, local_heads, HD),
        preferred_element_type=jnp.float32,
    )
    scores = jnp.concatenate([far_scores, near_scores], axis=-1) * score_scale
    scores = jnp.where(allowed[None], scores, -jnp.inf)
    row_top = jnp.max(scores, axis=-1, keepdims=True)
    weights = jnp.exp(scores - row_top)
    weights_bf = (weights / jnp.sum(weights, axis=-1, keepdims=True)).astype(jnp.bfloat16)
    mixed_heads = jnp.einsum(
        "hts,shd->thd", weights_bf, value_all, preferred_element_type=jnp.float32
    )
    attended = mixed_heads.astype(jnp.bfloat16).reshape(tok_count, local_width)
    partial_value = jnp.dot(attended, w_out, preferred_element_type=jnp.float32)
    down_o = jnp.einsum("td,rdk->trk", attended, sel_odown, preferred_element_type=jnp.float32)
    low_part = jnp.sum(down_o * member_f[:, :, None], axis=1)
    base_out, low_sum = tp_reduce_scatter(partial_value, low_part, "tp")
    low_o = low_sum.astype(jnp.bfloat16)
    spread_o = (pick_bf[:, :, None] * low_o[:, None, :]).reshape(tok_count, req_count * rank_dim)
    delta_o = jnp.dot(
        spread_o,
        sel_oup.reshape(req_count * rank_dim, local_width),
        preferred_element_type=jnp.float32,
    )
    own_rows = lax.dynamic_slice_in_dim(tokens, tp_id * local_width, local_width, 1).astype(
        jnp.float32
    )
    layer_out = (own_rows + base_out + delta_o).astype(jnp.bfloat16)
    page_row = page_table[0]
    page_count = page_row.shape[0]
    numbers = jnp.arange(page_count, dtype=jnp.int32)
    inverse = jnp.sum(jnp.where(page_row[:, None] == numbers[None, :], numbers[:, None], 0), axis=0)
    both_blocks = jnp.stack(
        [
            key_rows.reshape(page_count, PAGE, local_width),
            value_rows.reshape(page_count, PAGE, local_width),
        ],
        axis=1,
    )
    kv_pages = jnp.take(both_blocks, inverse, axis=0)
    return (layer_out, kv_pages)


def solution(mesh):
    return jax.shard_map(
        local,
        mesh=mesh,
        in_specs=(
            P("grp", None),
            P(),
            P(None, None, "tp"),
            P("tp", None),
            P("grp", "tp", None),
            P("grp", None, None, "tp"),
            P("grp", "tp", None),
            P("grp", None, "tp"),
            P(),
            P(),
            P(),
            P("grp", None),
        ),
        out_specs=(P("grp", "tp"), P("grp", None, None, "tp")),
        check_vma=False,
    )
```

```python
import math

import jax
import jax.numpy as jnp
from jax import lax
from jax.sharding import PartitionSpec as P

HD = 128
PAGE = 128


EPSILON = 1e-05
THETA = 10000.0


def shifted(block, axis, distance):
    devices = range(lax.axis_size(axis))
    route = [(i - distance, i) for i in devices if i - distance in devices]
    return lax.ppermute(block, axis, route)


USED = 16


def xor_allreduce(value, axis):
    count = lax.axis_size(axis)
    step = 1
    while step < count:
        route = [(i, i ^ step) for i in range(count)]
        value = value + lax.ppermute(value, axis, route)
        step *= 2
    return value


def xor_halving_sum(buf, axis):
    count = lax.axis_size(axis)
    me = lax.axis_index(axis)
    rows = buf.shape[0]
    cur = buf.reshape((count, -1))
    dists = []
    step = 1
    while step < count:
        dists.append(step)
        step *= 2
    for d in dists:
        bit = (me // d) % 2
        cur = cur.reshape((2, -1) + cur.shape[1:])
        keep = lax.dynamic_index_in_dim(cur, bit, 0, keepdims=False)
        send = lax.dynamic_index_in_dim(cur, 1 - bit, 0, keepdims=False)
        cur = keep + lax.ppermute(send, axis, [(i, i ^ d) for i in range(count)])
    for d in reversed(dists):
        bit = (me // d) % 2
        other = lax.ppermute(cur, axis, [(i, i ^ d) for i in range(count)])
        cur = jnp.where(bit == 0, jnp.stack([cur, other]), jnp.stack([other, cur]))
    return cur.reshape(buf.shape)


def radix_sum(buf, axis, inner):
    count = lax.axis_size(axis)
    outer = count // inner
    me = lax.axis_index(axis)
    lo = me % inner
    hi = me // inner

    def route(shift, size, stride):
        pairs = []
        for i in range(count):
            pos = (i // stride) % size
            pairs.append((i, i + (((pos + shift) % size) - pos) * stride))
        return pairs

    def scatter_step(value, own, size, stride):
        pieces = value.reshape((size, -1) + value.shape[1:])
        total = lax.dynamic_index_in_dim(pieces, own, 0, keepdims=False)
        for shift in range(1, size):
            part = lax.dynamic_index_in_dim(pieces, (own + shift) % size, 0, keepdims=False)
            total = total + lax.ppermute(part, axis, route(shift, size, stride))
        return total

    def gather_step(value, own, size, stride):
        got = [value]
        for shift in range(1, size):
            got.append(lax.ppermute(value, axis, route(shift, size, stride)))
        stack = jnp.stack(got)
        order = (own - jnp.arange(size, dtype=jnp.int32)) % size
        return jnp.take(stack, order, axis=0).reshape((-1,) + value.shape[1:])

    part = scatter_step(buf, lo, inner, 1)
    step = inner
    while step < count:
        part = part + lax.ppermute(part, axis, [(i, i ^ step) for i in range(count)])
        step *= 2
    return gather_step(part, lo, inner, 1)

def fetch_adapters(stores, req_adapter, holder, wanted, group_id):
    held = stores[0].shape[0]
    total = holder.shape[0]
    names = jnp.arange(total, dtype=jnp.int32)
    used = jnp.any(req_adapter.reshape(-1)[:, None] == names[None, :], axis=0)
    rank = jnp.cumsum(used.astype(jnp.int32)) - 1
    picks = jnp.arange(USED, dtype=jnp.int32)
    hit = used[None, :] & (rank[None, :] == picks[:, None])
    chosen = jnp.sum(jnp.where(hit, names[None, :], 0), axis=1)
    slots = holder[chosen]
    mine = (slots // held) == group_id
    local_idx = slots % held
    flat = jnp.concatenate([s.reshape(held, -1) for s in stores], axis=1)
    compact = jnp.zeros((USED, flat.shape[1]), flat.dtype)
    for h in range(held):
        take_h = (mine & (local_idx == h))[:, None]
        compact = jnp.where(take_h, flat[h][None, :], compact)
    compact = radix_sum(compact, "grp", 4)
    mine_rows = jnp.take(compact, rank[wanted], axis=0)
    out = []
    at = 0
    for s in stores:
        size = math.prod(s.shape[1:])
        out.append(mine_rows[:, at : at + size].reshape((wanted.shape[0],) + s.shape[1:]))
        at += size
    return tuple(out)


def rms_norm(token_rows, norm_gain):
    values = token_rows.astype(jnp.float32)
    norm_scale = lax.rsqrt(jnp.mean(values * values, axis=-1, keepdims=True) + EPSILON)
    return (values * norm_scale * norm_gain).astype(jnp.bfloat16)


def request_layout(lengths, offset, tok_count):
    end_at = jnp.cumsum(lengths)
    starts = end_at - lengths
    row_ids = jnp.arange(tok_count, dtype=jnp.int32)
    segment = jnp.sum((row_ids[:, None] >= end_at[None, :]).astype(jnp.int32), axis=1)
    member = segment[:, None] == jnp.arange(lengths.shape[0], dtype=jnp.int32)[None, :]
    begin_at = jnp.sum(jnp.where(member, starts[None, :], 0), axis=1)
    position = row_ids - begin_at + jnp.where(segment == 0, offset, 0)
    return (segment, member, position)


def rotate(head_rows, position, head_dim):
    half_dim = head_dim // 2
    frequency = THETA ** (-(jnp.arange(half_dim, dtype=jnp.float32) * (2.0 / head_dim)))
    angles = position.astype(jnp.float32)[:, None] * frequency[None, :]
    cosine = jnp.cos(angles)[:, None, :]
    sine_part = jnp.sin(angles)[:, None, :]
    lower_half = head_rows[..., :half_dim]
    upper_half = head_rows[..., half_dim:]
    return jnp.concatenate(
        [
            lower_half * cosine - upper_half * sine_part,
            upper_half * cosine + lower_half * sine_part,
        ],
        axis=-1,
    )


def local(
    tokens,
    norm_gain,
    w_qkv,
    w_out,
    a_in,
    b_in,
    a_out,
    b_out,
    req_len,
    req_adapter,
    holder,
    page_table,
):
    tok_count = tokens.shape[0]
    local_width = w_out.shape[0]
    local_heads = local_width // HD
    req_count = req_len.shape[1]
    rank_dim = a_out.shape[2]
    group_id = lax.axis_index("grp")
    tp_id = lax.axis_index("tp")
    lengths = lax.dynamic_index_in_dim(req_len, group_id, 0, keepdims=False)
    earlier = lax.dynamic_index_in_dim(req_len, jnp.maximum(group_id - 1, 0), 0, keepdims=False)
    continued = group_id > 0
    prev_len = earlier[req_count - 1]
    offset = jnp.where(continued, prev_len, 0)
    segment, member, position = request_layout(lengths, offset, tok_count)
    wanted = lax.dynamic_index_in_dim(req_adapter, group_id, 0, keepdims=False)
    sel_in, sel_up, sel_odown, sel_oup = fetch_adapters(
        (a_in, b_in, a_out, b_out), req_adapter, holder, wanted, group_id
    )
    member_f = member.astype(jnp.float32)
    pick_bf = member.astype(jnp.bfloat16)
    normed = rms_norm(tokens, norm_gain)
    own_cols = lax.dynamic_slice_in_dim(normed, tp_id * local_width, local_width, 1)
    down_f = jnp.einsum("td,rdk->trk", own_cols, sel_in, preferred_element_type=jnp.float32)
    lowrank_f = xor_allreduce(jnp.sum(down_f * member_f[:, :, None], axis=1), "tp")
    lowrank = lowrank_f.astype(jnp.bfloat16)
    spread = (pick_bf[:, :, None] * lowrank[:, None, :]).reshape(tok_count, req_count, 3, rank_dim)
    delta_qkv = jnp.einsum("trck,rckd->tcd", spread, sel_up, preferred_element_type=jnp.float32)
    base_qkv = jnp.dot(
        normed, w_qkv.reshape(w_qkv.shape[0], 3 * local_width), preferred_element_type=jnp.float32
    )
    qkv = (base_qkv.reshape(tok_count, 3, local_width) + delta_qkv).reshape(
        tok_count, 3, local_heads, HD
    )
    query_rows = rotate(qkv[:, 0], position, HD).astype(jnp.bfloat16)
    key_rows = rotate(qkv[:, 1], position, HD).astype(jnp.bfloat16).reshape(tok_count, local_width)
    value_rows = qkv[:, 2].astype(jnp.bfloat16).reshape(tok_count, local_width)
    row_ids = jnp.arange(tok_count, dtype=jnp.int32)
    far_key, far_value = shifted((key_rows, value_rows), "grp", 1)
    far_ok = continued & (segment[:, None] == 0) & (row_ids[None, :] >= tok_count - prev_len)
    far_count = far_key.shape[0]
    near_ok = (segment[:, None] == segment[None, :]) & (row_ids[None, :] <= row_ids[:, None])
    score_scale = 1.0 / math.sqrt(HD)
    far_heads = far_key.reshape(far_count, local_heads, HD)
    near_heads = key_rows.reshape(tok_count, local_heads, HD)
    chunks = 2
    size = tok_count // chunks
    attended_parts = []
    base_parts = []
    for c in range(chunks):
        lo = c * size
        hi = lo + size
        q_c = query_rows[lo:hi]
        near_scores = jnp.einsum(
            "thd,shd->hts", q_c, near_heads[:hi], preferred_element_type=jnp.float32
        )
        far_scores = jnp.einsum(
            "thd,shd->hts", q_c, far_heads, preferred_element_type=jnp.float32
        )
        allowed = jnp.concatenate([far_ok[lo:hi], near_ok[lo:hi, :hi]], axis=1)
        scores = jnp.concatenate([far_scores, near_scores], axis=-1) * score_scale
        scores = jnp.where(allowed[None], scores, -jnp.inf)
        row_top = jnp.max(scores, axis=-1, keepdims=True)
        weights = jnp.exp(scores - row_top)
        weights_bf = (weights / jnp.sum(weights, axis=-1, keepdims=True)).astype(jnp.bfloat16)
        value_c = jnp.concatenate([far_value, value_rows[:hi]], axis=0).reshape(
            far_count + hi, local_heads, HD
        )
        mixed_heads = jnp.einsum(
            "hts,shd->thd", weights_bf, value_c, preferred_element_type=jnp.float32
        )
        attended_c = mixed_heads.astype(jnp.bfloat16).reshape(size, local_width)
        partial_c = jnp.dot(attended_c, w_out, preferred_element_type=jnp.float32)
        base_parts.append(
            lax.psum_scatter(
                partial_c.astype(jnp.bfloat16), "tp", scatter_dimension=1, tiled=True
            ).astype(jnp.float32)
        )
        attended_parts.append(attended_c)
    attended = jnp.concatenate(attended_parts, axis=0)
    base_out = jnp.concatenate(base_parts, axis=0)
    down_o = jnp.einsum("td,rdk->trk", attended, sel_odown, preferred_element_type=jnp.float32)
    low_part = jnp.sum(down_o * member_f[:, :, None], axis=1).astype(jnp.bfloat16)
    low_o = xor_allreduce(low_part, "tp")
    spread_o = (pick_bf[:, :, None] * low_o[:, None, :]).reshape(tok_count, req_count * rank_dim)
    delta_o = jnp.dot(
        spread_o,
        sel_oup.reshape(req_count * rank_dim, local_width),
        preferred_element_type=jnp.float32,
    )
    own_rows = lax.dynamic_slice_in_dim(tokens, tp_id * local_width, local_width, 1).astype(
        jnp.float32
    )
    layer_out = (own_rows + base_out + delta_o).astype(jnp.bfloat16)
    page_row = page_table[0]
    page_count = page_row.shape[0]
    numbers = jnp.arange(page_count, dtype=jnp.int32)
    inverse = jnp.sum(jnp.where(page_row[:, None] == numbers[None, :], numbers[:, None], 0), axis=0)
    both_blocks = jnp.stack(
        [
            key_rows.reshape(page_count, PAGE, local_width),
            value_rows.reshape(page_count, PAGE, local_width),
        ],
        axis=1,
    )
    kv_pages = jnp.take(both_blocks, inverse, axis=0)
    return (layer_out, kv_pages)


def solution(mesh):
    return jax.shard_map(
        local,
        mesh=mesh,
        in_specs=(
            P("grp", None),
            P(),
            P(None, None, "tp"),
            P("tp", None),
            P("grp", "tp", None),
            P("grp", None, None, "tp"),
            P("grp", "tp", None),
            P("grp", None, "tp"),
            P(),
            P(),
            P(),
            P("grp", None),
        ),
        out_specs=(P("grp", "tp"), P("grp", None, None, "tp")),
        check_vma=False,
    )
```

```python
import math

import jax
import jax.numpy as jnp
from jax import lax
from jax.sharding import PartitionSpec as P

HD = 128
PAGE = 128


EPSILON = 1e-05
THETA = 10000.0


def shifted(block, axis, distance):
    devices = range(lax.axis_size(axis))
    route = [(i - distance, i) for i in devices if i - distance in devices]
    return lax.ppermute(block, axis, route)


USED = 16


def xor_allreduce(value, axis):
    count = lax.axis_size(axis)
    step = 1
    while step < count:
        route = [(i, i ^ step) for i in range(count)]
        value = value + lax.ppermute(value, axis, route)
        step *= 2
    return value


def xor_halving_sum(buf, axis):
    count = lax.axis_size(axis)
    me = lax.axis_index(axis)
    rows = buf.shape[0]
    cur = buf.reshape((count, -1))
    dists = []
    step = 1
    while step < count:
        dists.append(step)
        step *= 2
    for d in dists:
        bit = (me // d) % 2
        cur = cur.reshape((2, -1) + cur.shape[1:])
        keep = lax.dynamic_index_in_dim(cur, bit, 0, keepdims=False)
        send = lax.dynamic_index_in_dim(cur, 1 - bit, 0, keepdims=False)
        cur = keep + lax.ppermute(send, axis, [(i, i ^ d) for i in range(count)])
    for d in reversed(dists):
        bit = (me // d) % 2
        other = lax.ppermute(cur, axis, [(i, i ^ d) for i in range(count)])
        cur = jnp.where(bit == 0, jnp.stack([cur, other]), jnp.stack([other, cur]))
    return cur.reshape(buf.shape)


def radix_sum(buf, axis, inner):
    count = lax.axis_size(axis)
    outer = count // inner
    me = lax.axis_index(axis)
    lo = me % inner
    hi = me // inner

    def route(shift, size, stride):
        pairs = []
        for i in range(count):
            pos = (i // stride) % size
            pairs.append((i, i + (((pos + shift) % size) - pos) * stride))
        return pairs

    def scatter_step(value, own, size, stride):
        pieces = value.reshape((size, -1) + value.shape[1:])
        total = lax.dynamic_index_in_dim(pieces, own, 0, keepdims=False)
        for shift in range(1, size):
            part = lax.dynamic_index_in_dim(pieces, (own + shift) % size, 0, keepdims=False)
            total = total + lax.ppermute(part, axis, route(shift, size, stride))
        return total

    def gather_step(value, own, size, stride):
        got = [value]
        for shift in range(1, size):
            got.append(lax.ppermute(value, axis, route(shift, size, stride)))
        stack = jnp.stack(got)
        order = (own - jnp.arange(size, dtype=jnp.int32)) % size
        return jnp.take(stack, order, axis=0).reshape((-1,) + value.shape[1:])

    part = scatter_step(buf, lo, inner, 1)
    step = inner
    while step < count:
        part = part + lax.ppermute(part, axis, [(i, i ^ step) for i in range(count)])
        step *= 2
    return gather_step(part, lo, inner, 1)

def fetch_adapters(stores, req_adapter, holder, wanted, group_id):
    held = stores[0].shape[0]
    total = holder.shape[0]
    names = jnp.arange(total, dtype=jnp.int32)
    used = jnp.any(req_adapter.reshape(-1)[:, None] == names[None, :], axis=0)
    rank = jnp.cumsum(used.astype(jnp.int32)) - 1
    picks = jnp.arange(USED, dtype=jnp.int32)
    hit = used[None, :] & (rank[None, :] == picks[:, None])
    chosen = jnp.sum(jnp.where(hit, names[None, :], 0), axis=1)
    slots = holder[chosen]
    mine = (slots // held) == group_id
    local_idx = slots % held
    flat = jnp.concatenate([s.reshape(held, -1) for s in stores], axis=1)
    compact = jnp.zeros((USED, flat.shape[1]), flat.dtype)
    for h in range(held):
        take_h = (mine & (local_idx == h))[:, None]
        compact = jnp.where(take_h, flat[h][None, :], compact)
    compact = radix_sum(compact, "grp", 4)
    mine_rows = jnp.take(compact, rank[wanted], axis=0)
    out = []
    at = 0
    for s in stores:
        size = math.prod(s.shape[1:])
        out.append(mine_rows[:, at : at + size].reshape((wanted.shape[0],) + s.shape[1:]))
        at += size
    return tuple(out)


def rms_norm(token_rows, norm_gain):
    values = token_rows.astype(jnp.float32)
    norm_scale = lax.rsqrt(jnp.mean(values * values, axis=-1, keepdims=True) + EPSILON)
    return (values * norm_scale * norm_gain).astype(jnp.bfloat16)


def request_layout(lengths, offset, tok_count):
    end_at = jnp.cumsum(lengths)
    starts = end_at - lengths
    row_ids = jnp.arange(tok_count, dtype=jnp.int32)
    segment = jnp.sum((row_ids[:, None] >= end_at[None, :]).astype(jnp.int32), axis=1)
    member = segment[:, None] == jnp.arange(lengths.shape[0], dtype=jnp.int32)[None, :]
    begin_at = jnp.sum(jnp.where(member, starts[None, :], 0), axis=1)
    position = row_ids - begin_at + jnp.where(segment == 0, offset, 0)
    return (segment, member, position)


def rotate(head_rows, position, head_dim):
    half_dim = head_dim // 2
    frequency = THETA ** (-(jnp.arange(half_dim, dtype=jnp.float32) * (2.0 / head_dim)))
    angles = position.astype(jnp.float32)[:, None] * frequency[None, :]
    cosine = jnp.cos(angles)[:, None, :]
    sine_part = jnp.sin(angles)[:, None, :]
    lower_half = head_rows[..., :half_dim]
    upper_half = head_rows[..., half_dim:]
    return jnp.concatenate(
        [
            lower_half * cosine - upper_half * sine_part,
            upper_half * cosine + lower_half * sine_part,
        ],
        axis=-1,
    )


def local(
    tokens,
    norm_gain,
    w_qkv,
    w_out,
    a_in,
    b_in,
    a_out,
    b_out,
    req_len,
    req_adapter,
    holder,
    page_table,
):
    tok_count = tokens.shape[0]
    local_width = w_out.shape[0]
    local_heads = local_width // HD
    req_count = req_len.shape[1]
    rank_dim = a_out.shape[2]
    group_id = lax.axis_index("grp")
    tp_id = lax.axis_index("tp")
    lengths = lax.dynamic_index_in_dim(req_len, group_id, 0, keepdims=False)
    earlier = lax.dynamic_index_in_dim(req_len, jnp.maximum(group_id - 1, 0), 0, keepdims=False)
    continued = group_id > 0
    prev_len = earlier[req_count - 1]
    offset = jnp.where(continued, prev_len, 0)
    segment, member, position = request_layout(lengths, offset, tok_count)
    wanted = lax.dynamic_index_in_dim(req_adapter, group_id, 0, keepdims=False)
    sel_in, sel_up, sel_odown, sel_oup = fetch_adapters(
        (a_in, b_in, a_out, b_out), req_adapter, holder, wanted, group_id
    )
    member_f = member.astype(jnp.float32)
    pick_bf = member.astype(jnp.bfloat16)
    normed = rms_norm(tokens, norm_gain)
    own_cols = lax.dynamic_slice_in_dim(normed, tp_id * local_width, local_width, 1)
    down_f = jnp.einsum("td,rdk->trk", own_cols, sel_in, preferred_element_type=jnp.float32)
    lowrank_f = xor_allreduce(jnp.sum(down_f * member_f[:, :, None], axis=1), "tp")
    lowrank = lowrank_f.astype(jnp.bfloat16)
    spread = (pick_bf[:, :, None] * lowrank[:, None, :]).reshape(tok_count, req_count, 3, rank_dim)
    delta_qkv = jnp.einsum("trck,rckd->tcd", spread, sel_up, preferred_element_type=jnp.float32)
    base_qkv = jnp.dot(
        normed, w_qkv.reshape(w_qkv.shape[0], 3 * local_width), preferred_element_type=jnp.float32
    )
    qkv = (base_qkv.reshape(tok_count, 3, local_width) + delta_qkv).reshape(
        tok_count, 3, local_heads, HD
    )
    query_rows = rotate(qkv[:, 0], position, HD).astype(jnp.bfloat16)
    key_rows = rotate(qkv[:, 1], position, HD).astype(jnp.bfloat16).reshape(tok_count, local_width)
    value_rows = qkv[:, 2].astype(jnp.bfloat16).reshape(tok_count, local_width)
    row_ids = jnp.arange(tok_count, dtype=jnp.int32)
    far_key, far_value = shifted((key_rows, value_rows), "grp", 1)
    far_ok = continued & (segment[:, None] == 0) & (row_ids[None, :] >= tok_count - prev_len)
    far_count = far_key.shape[0]
    near_ok = (segment[:, None] == segment[None, :]) & (row_ids[None, :] <= row_ids[:, None])
    score_scale = 1.0 / math.sqrt(HD)
    far_heads = far_key.reshape(far_count, local_heads, HD)
    near_heads = key_rows.reshape(tok_count, local_heads, HD)
    chunks = 1
    size = tok_count // chunks
    attended_parts = []
    base_parts = []
    for c in range(chunks):
        lo = c * size
        hi = lo + size
        q_c = query_rows[lo:hi]
        near_scores = jnp.einsum(
            "thd,shd->hts", q_c, near_heads[:hi], preferred_element_type=jnp.float32
        )
        far_scores = jnp.einsum(
            "thd,shd->hts", q_c, far_heads, preferred_element_type=jnp.float32
        )
        allowed = jnp.concatenate([far_ok[lo:hi], near_ok[lo:hi, :hi]], axis=1)
        scores = jnp.concatenate([far_scores, near_scores], axis=-1) * score_scale
        scores = jnp.where(allowed[None], scores, -jnp.inf)
        row_top = jnp.max(scores, axis=-1, keepdims=True)
        weights = jnp.exp(scores - row_top)
        weights_bf = (weights / jnp.sum(weights, axis=-1, keepdims=True)).astype(jnp.bfloat16)
        value_c = jnp.concatenate([far_value, value_rows[:hi]], axis=0).reshape(
            far_count + hi, local_heads, HD
        )
        mixed_heads = jnp.einsum(
            "hts,shd->thd", weights_bf, value_c, preferred_element_type=jnp.float32
        )
        attended_c = mixed_heads.astype(jnp.bfloat16).reshape(size, local_width)
        partial_c = jnp.dot(attended_c, w_out, preferred_element_type=jnp.float32)
        base_parts.append(
            lax.psum_scatter(
                partial_c.astype(jnp.bfloat16), "tp", scatter_dimension=1, tiled=True
            ).astype(jnp.float32)
        )
        attended_parts.append(attended_c)
    attended = jnp.concatenate(attended_parts, axis=0)
    base_out = jnp.concatenate(base_parts, axis=0)
    down_o = jnp.einsum("td,rdk->trk", attended, sel_odown, preferred_element_type=jnp.float32)
    low_part = jnp.sum(down_o * member_f[:, :, None], axis=1).astype(jnp.bfloat16)
    low_o = xor_allreduce(low_part, "tp")
    spread_o = (pick_bf[:, :, None] * low_o[:, None, :]).reshape(tok_count, req_count * rank_dim)
    delta_o = jnp.dot(
        spread_o,
        sel_oup.reshape(req_count * rank_dim, local_width),
        preferred_element_type=jnp.float32,
    )
    own_rows = lax.dynamic_slice_in_dim(tokens, tp_id * local_width, local_width, 1).astype(
        jnp.float32
    )
    layer_out = (own_rows + base_out + delta_o).astype(jnp.bfloat16)
    page_row = page_table[0]
    page_count = page_row.shape[0]
    numbers = jnp.arange(page_count, dtype=jnp.int32)
    inverse = jnp.sum(jnp.where(page_row[:, None] == numbers[None, :], numbers[:, None], 0), axis=0)
    both_blocks = jnp.stack(
        [
            key_rows.reshape(page_count, PAGE, local_width),
            value_rows.reshape(page_count, PAGE, local_width),
        ],
        axis=1,
    )
    kv_pages = jnp.take(both_blocks, inverse, axis=0)
    return (layer_out, kv_pages)


def solution(mesh):
    return jax.shard_map(
        local,
        mesh=mesh,
        in_specs=(
            P("grp", None),
            P(),
            P(None, None, "tp"),
            P("tp", None),
            P("grp", "tp", None),
            P("grp", None, None, "tp"),
            P("grp", "tp", None),
            P("grp", None, "tp"),
            P(),
            P(),
            P(),
            P("grp", None),
        ),
        out_specs=(P("grp", "tp"), P("grp", None, None, "tp")),
        check_vma=False,
    )
```

```python
import math

import jax
import jax.numpy as jnp
from jax import lax
from jax.sharding import PartitionSpec as P

HD = 128
PAGE = 128


EPSILON = 1e-05
THETA = 10000.0


def shifted(block, axis, distance):
    devices = range(lax.axis_size(axis))
    route = [(i - distance, i) for i in devices if i - distance in devices]
    return lax.ppermute(block, axis, route)


USED = 16


def xor_allreduce(value, axis):
    count = lax.axis_size(axis)
    step = 1
    while step < count:
        route = [(i, i ^ step) for i in range(count)]
        value = value + lax.ppermute(value, axis, route)
        step *= 2
    return value


def xor_halving_sum(buf, axis):
    count = lax.axis_size(axis)
    me = lax.axis_index(axis)
    rows = buf.shape[0]
    cur = buf.reshape((count, -1))
    dists = []
    step = 1
    while step < count:
        dists.append(step)
        step *= 2
    for d in dists:
        bit = (me // d) % 2
        cur = cur.reshape((2, -1) + cur.shape[1:])
        keep = lax.dynamic_index_in_dim(cur, bit, 0, keepdims=False)
        send = lax.dynamic_index_in_dim(cur, 1 - bit, 0, keepdims=False)
        cur = keep + lax.ppermute(send, axis, [(i, i ^ d) for i in range(count)])
    for d in reversed(dists):
        bit = (me // d) % 2
        other = lax.ppermute(cur, axis, [(i, i ^ d) for i in range(count)])
        cur = jnp.where(bit == 0, jnp.stack([cur, other]), jnp.stack([other, cur]))
    return cur.reshape(buf.shape)


def radix_sum(buf, axis, inner):
    count = lax.axis_size(axis)
    outer = count // inner
    me = lax.axis_index(axis)
    lo = me % inner
    hi = me // inner

    def route(shift, size, stride):
        pairs = []
        for i in range(count):
            pos = (i // stride) % size
            pairs.append((i, i + (((pos + shift) % size) - pos) * stride))
        return pairs

    def scatter_step(value, own, size, stride):
        pieces = value.reshape((size, -1) + value.shape[1:])
        total = lax.dynamic_index_in_dim(pieces, own, 0, keepdims=False)
        for shift in range(1, size):
            part = lax.dynamic_index_in_dim(pieces, (own + shift) % size, 0, keepdims=False)
            total = total + lax.ppermute(part, axis, route(shift, size, stride))
        return total

    def gather_step(value, own, size, stride):
        got = [value]
        for shift in range(1, size):
            got.append(lax.ppermute(value, axis, route(shift, size, stride)))
        stack = jnp.stack(got)
        order = (own - jnp.arange(size, dtype=jnp.int32)) % size
        return jnp.take(stack, order, axis=0).reshape((-1,) + value.shape[1:])

    part = scatter_step(buf, lo, inner, 1)
    step = inner
    while step < count:
        part = part + lax.ppermute(part, axis, [(i, i ^ step) for i in range(count)])
        step *= 2
    return gather_step(part, lo, inner, 1)

def project_scatter(attended, w_out, axis):
    count = lax.axis_size(axis)
    me = lax.axis_index(axis)
    core = me % 2
    chip = me // 2
    chips = count // 2
    rows, width = w_out.shape
    part_w = width // count
    w4 = w_out.reshape(rows, chips, 2, part_w)
    w_own = lax.dynamic_index_in_dim(w4, core, 2, keepdims=False)
    w_away = lax.dynamic_index_in_dim(w4, 1 - core, 2, keepdims=False)
    own = jnp.einsum("td,dcw->ctw", attended, w_own, preferred_element_type=jnp.float32)
    away = jnp.einsum("td,dcw->ctw", attended, w_away, preferred_element_type=jnp.float32)
    got = lax.ppermute(away.astype(jnp.bfloat16), axis, [(i, i ^ 1) for i in range(count)])
    chip_sum = own.astype(jnp.bfloat16).astype(jnp.float32) + got.astype(jnp.float32)
    total = lax.dynamic_index_in_dim(chip_sum, chip, 0, keepdims=False)
    for shift in range(1, chips):
        piece = lax.dynamic_index_in_dim(chip_sum, (chip + shift) % chips, 0, keepdims=False)
        route = [(i, ((i // 2 + shift) % chips) * 2 + i % 2) for i in range(count)]
        total = total + lax.ppermute(piece.astype(jnp.bfloat16), axis, route).astype(jnp.float32)
    return total


def fetch_adapters(stores, req_adapter, holder, wanted, group_id):
    held = stores[0].shape[0]
    total = holder.shape[0]
    names = jnp.arange(total, dtype=jnp.int32)
    used = jnp.any(req_adapter.reshape(-1)[:, None] == names[None, :], axis=0)
    rank = jnp.cumsum(used.astype(jnp.int32)) - 1
    picks = jnp.arange(USED, dtype=jnp.int32)
    hit = used[None, :] & (rank[None, :] == picks[:, None])
    chosen = jnp.sum(jnp.where(hit, names[None, :], 0), axis=1)
    slots = holder[chosen]
    mine = (slots // held) == group_id
    local_idx = slots % held
    flat = jnp.concatenate([s.reshape(held, -1) for s in stores], axis=1)
    compact = jnp.zeros((USED, flat.shape[1]), flat.dtype)
    for h in range(held):
        take_h = (mine & (local_idx == h))[:, None]
        compact = jnp.where(take_h, flat[h][None, :], compact)
    compact = radix_sum(compact, "grp", 4)
    mine_rows = jnp.take(compact, rank[wanted], axis=0)
    out = []
    at = 0
    for s in stores:
        size = math.prod(s.shape[1:])
        out.append(mine_rows[:, at : at + size].reshape((wanted.shape[0],) + s.shape[1:]))
        at += size
    return tuple(out)


def rms_norm(token_rows, norm_gain):
    values = token_rows.astype(jnp.float32)
    norm_scale = lax.rsqrt(jnp.mean(values * values, axis=-1, keepdims=True) + EPSILON)
    return (values * norm_scale * norm_gain).astype(jnp.bfloat16)


def request_layout(lengths, offset, tok_count):
    end_at = jnp.cumsum(lengths)
    starts = end_at - lengths
    row_ids = jnp.arange(tok_count, dtype=jnp.int32)
    segment = jnp.sum((row_ids[:, None] >= end_at[None, :]).astype(jnp.int32), axis=1)
    member = segment[:, None] == jnp.arange(lengths.shape[0], dtype=jnp.int32)[None, :]
    begin_at = jnp.sum(jnp.where(member, starts[None, :], 0), axis=1)
    position = row_ids - begin_at + jnp.where(segment == 0, offset, 0)
    return (segment, member, position)


def rotate(head_rows, position, head_dim):
    half_dim = head_dim // 2
    frequency = THETA ** (-(jnp.arange(half_dim, dtype=jnp.float32) * (2.0 / head_dim)))
    angles = position.astype(jnp.float32)[:, None] * frequency[None, :]
    cosine = jnp.cos(angles)[:, None, :]
    sine_part = jnp.sin(angles)[:, None, :]
    lower_half = head_rows[..., :half_dim]
    upper_half = head_rows[..., half_dim:]
    return jnp.concatenate(
        [
            lower_half * cosine - upper_half * sine_part,
            upper_half * cosine + lower_half * sine_part,
        ],
        axis=-1,
    )


def local(
    tokens,
    norm_gain,
    w_qkv,
    w_out,
    a_in,
    b_in,
    a_out,
    b_out,
    req_len,
    req_adapter,
    holder,
    page_table,
):
    tok_count = tokens.shape[0]
    local_width = w_out.shape[0]
    local_heads = local_width // HD
    req_count = req_len.shape[1]
    rank_dim = a_out.shape[2]
    group_id = lax.axis_index("grp")
    tp_id = lax.axis_index("tp")
    lengths = lax.dynamic_index_in_dim(req_len, group_id, 0, keepdims=False)
    earlier = lax.dynamic_index_in_dim(req_len, jnp.maximum(group_id - 1, 0), 0, keepdims=False)
    continued = group_id > 0
    prev_len = earlier[req_count - 1]
    offset = jnp.where(continued, prev_len, 0)
    segment, member, position = request_layout(lengths, offset, tok_count)
    wanted = lax.dynamic_index_in_dim(req_adapter, group_id, 0, keepdims=False)
    sel_in, sel_up, sel_odown, sel_oup = fetch_adapters(
        (a_in, b_in, a_out, b_out), req_adapter, holder, wanted, group_id
    )
    member_f = member.astype(jnp.float32)
    pick_bf = member.astype(jnp.bfloat16)
    normed = rms_norm(tokens, norm_gain)
    own_cols = lax.dynamic_slice_in_dim(normed, tp_id * local_width, local_width, 1)
    down_f = jnp.einsum("td,rdk->trk", own_cols, sel_in, preferred_element_type=jnp.float32)
    lowrank_f = xor_allreduce(jnp.sum(down_f * member_f[:, :, None], axis=1), "tp")
    lowrank = lowrank_f.astype(jnp.bfloat16)
    spread = (pick_bf[:, :, None] * lowrank[:, None, :]).reshape(tok_count, req_count, 3, rank_dim)
    delta_qkv = jnp.einsum("trck,rckd->tcd", spread, sel_up, preferred_element_type=jnp.float32)
    base_qkv = jnp.dot(
        normed, w_qkv.reshape(w_qkv.shape[0], 3 * local_width), preferred_element_type=jnp.float32
    )
    qkv = (base_qkv.reshape(tok_count, 3, local_width) + delta_qkv).reshape(
        tok_count, 3, local_heads, HD
    )
    query_rows = rotate(qkv[:, 0], position, HD).astype(jnp.bfloat16)
    key_rows = rotate(qkv[:, 1], position, HD).astype(jnp.bfloat16).reshape(tok_count, local_width)
    value_rows = qkv[:, 2].astype(jnp.bfloat16).reshape(tok_count, local_width)
    row_ids = jnp.arange(tok_count, dtype=jnp.int32)
    far_key, far_value = shifted((key_rows, value_rows), "grp", 1)
    far_ok = continued & (segment[:, None] == 0) & (row_ids[None, :] >= tok_count - prev_len)
    far_count = far_key.shape[0]
    near_ok = (segment[:, None] == segment[None, :]) & (row_ids[None, :] <= row_ids[:, None])
    score_scale = 1.0 / math.sqrt(HD)
    far_heads = far_key.reshape(far_count, local_heads, HD)
    near_heads = key_rows.reshape(tok_count, local_heads, HD)
    chunks = 1
    size = tok_count // chunks
    attended_parts = []
    base_parts = []
    for c in range(chunks):
        lo = c * size
        hi = lo + size
        q_c = query_rows[lo:hi]
        near_scores = jnp.einsum(
            "thd,shd->hts", q_c, near_heads[:hi], preferred_element_type=jnp.float32
        )
        far_scores = jnp.einsum(
            "thd,shd->hts", q_c, far_heads, preferred_element_type=jnp.float32
        )
        allowed = jnp.concatenate([far_ok[lo:hi], near_ok[lo:hi, :hi]], axis=1)
        scores = jnp.concatenate([far_scores, near_scores], axis=-1) * score_scale
        scores = jnp.where(allowed[None], scores, -jnp.inf)
        row_top = jnp.max(scores, axis=-1, keepdims=True)
        weights = jnp.exp(scores - row_top)
        weights_bf = (weights / jnp.sum(weights, axis=-1, keepdims=True)).astype(jnp.bfloat16)
        value_c = jnp.concatenate([far_value, value_rows[:hi]], axis=0).reshape(
            far_count + hi, local_heads, HD
        )
        mixed_heads = jnp.einsum(
            "hts,shd->thd", weights_bf, value_c, preferred_element_type=jnp.float32
        )
        attended_c = mixed_heads.astype(jnp.bfloat16).reshape(size, local_width)
        base_parts.append(project_scatter(attended_c, w_out, "tp"))
        attended_parts.append(attended_c)
    attended = jnp.concatenate(attended_parts, axis=0)
    base_out = jnp.concatenate(base_parts, axis=0)
    down_o = jnp.einsum("td,rdk->trk", attended, sel_odown, preferred_element_type=jnp.float32)
    low_part = jnp.sum(down_o * member_f[:, :, None], axis=1).astype(jnp.bfloat16)
    low_o = xor_allreduce(low_part, "tp")
    spread_o = (pick_bf[:, :, None] * low_o[:, None, :]).reshape(tok_count, req_count * rank_dim)
    delta_o = jnp.dot(
        spread_o,
        sel_oup.reshape(req_count * rank_dim, local_width),
        preferred_element_type=jnp.float32,
    )
    own_rows = lax.dynamic_slice_in_dim(tokens, tp_id * local_width, local_width, 1).astype(
        jnp.float32
    )
    layer_out = (own_rows + base_out + delta_o).astype(jnp.bfloat16)
    page_row = page_table[0]
    page_count = page_row.shape[0]
    numbers = jnp.arange(page_count, dtype=jnp.int32)
    inverse = jnp.sum(jnp.where(page_row[:, None] == numbers[None, :], numbers[:, None], 0), axis=0)
    both_blocks = jnp.stack(
        [
            key_rows.reshape(page_count, PAGE, local_width),
            value_rows.reshape(page_count, PAGE, local_width),
        ],
        axis=1,
    )
    kv_pages = jnp.take(both_blocks, inverse, axis=0)
    return (layer_out, kv_pages)


def solution(mesh):
    return jax.shard_map(
        local,
        mesh=mesh,
        in_specs=(
            P("grp", None),
            P(),
            P(None, None, "tp"),
            P("tp", None),
            P("grp", "tp", None),
            P("grp", None, None, "tp"),
            P("grp", "tp", None),
            P("grp", None, "tp"),
            P(),
            P(),
            P(),
            P("grp", None),
        ),
        out_specs=(P("grp", "tp"), P("grp", None, None, "tp")),
        check_vma=False,
    )
```

```python
import math

import jax
import jax.numpy as jnp
from jax import lax
from jax.sharding import PartitionSpec as P

HD = 128
PAGE = 128


EPSILON = 1e-05
THETA = 10000.0


def shifted(block, axis, distance):
    devices = range(lax.axis_size(axis))
    route = [(i - distance, i) for i in devices if i - distance in devices]
    return lax.ppermute(block, axis, route)


USED = 16


def xor_allreduce(value, axis):
    count = lax.axis_size(axis)
    step = 1
    while step < count:
        route = [(i, i ^ step) for i in range(count)]
        value = value + lax.ppermute(value, axis, route)
        step *= 2
    return value


def xor_halving_sum(buf, axis):
    count = lax.axis_size(axis)
    me = lax.axis_index(axis)
    rows = buf.shape[0]
    cur = buf.reshape((count, -1))
    dists = []
    step = 1
    while step < count:
        dists.append(step)
        step *= 2
    for d in dists:
        bit = (me // d) % 2
        cur = cur.reshape((2, -1) + cur.shape[1:])
        keep = lax.dynamic_index_in_dim(cur, bit, 0, keepdims=False)
        send = lax.dynamic_index_in_dim(cur, 1 - bit, 0, keepdims=False)
        cur = keep + lax.ppermute(send, axis, [(i, i ^ d) for i in range(count)])
    for d in reversed(dists):
        bit = (me // d) % 2
        other = lax.ppermute(cur, axis, [(i, i ^ d) for i in range(count)])
        cur = jnp.where(bit == 0, jnp.stack([cur, other]), jnp.stack([other, cur]))
    return cur.reshape(buf.shape)


def radix_sum(buf, axis, inner):
    count = lax.axis_size(axis)
    outer = count // inner
    me = lax.axis_index(axis)
    lo = me % inner
    hi = me // inner

    def route(shift, size, stride):
        pairs = []
        for i in range(count):
            pos = (i // stride) % size
            pairs.append((i, i + (((pos + shift) % size) - pos) * stride))
        return pairs

    def scatter_step(value, own, size, stride):
        pieces = value.reshape((size, -1) + value.shape[1:])
        total = lax.dynamic_index_in_dim(pieces, own, 0, keepdims=False)
        for shift in range(1, size):
            part = lax.dynamic_index_in_dim(pieces, (own + shift) % size, 0, keepdims=False)
            total = total + lax.ppermute(part, axis, route(shift, size, stride))
        return total

    def gather_step(value, own, size, stride):
        got = [value]
        for shift in range(1, size):
            got.append(lax.ppermute(value, axis, route(shift, size, stride)))
        stack = jnp.stack(got)
        order = (own - jnp.arange(size, dtype=jnp.int32)) % size
        return jnp.take(stack, order, axis=0).reshape((-1,) + value.shape[1:])

    part = scatter_step(buf, lo, inner, 1)
    step = inner
    while step < count:
        part = part + lax.ppermute(part, axis, [(i, i ^ step) for i in range(count)])
        step *= 2
    return gather_step(part, lo, inner, 1)

def project_scatter(attended, w_out, low, axis):
    count = lax.axis_size(axis)
    me = lax.axis_index(axis)
    core = me % 2
    chip = me // 2
    chips = count // 2
    rows, width = w_out.shape
    tok = attended.shape[0]
    part_w = width // count
    w4 = w_out.reshape(rows, chips, 2, part_w)
    w_own = lax.dynamic_index_in_dim(w4, core, 2, keepdims=False)
    w_away = lax.dynamic_index_in_dim(w4, 1 - core, 2, keepdims=False)
    own = jnp.einsum("td,dcw->ctw", attended, w_own, preferred_element_type=jnp.float32)
    away = jnp.einsum("td,dcw->ctw", attended, w_away, preferred_element_type=jnp.float32)
    low_rows = low.astype(jnp.bfloat16).reshape(-1, part_w)
    msg = jnp.concatenate([away.astype(jnp.bfloat16).reshape(chips * tok, part_w), low_rows], axis=0)
    got = lax.ppermute(msg, axis, [(i, i ^ 1) for i in range(count)])
    chip_sum = own.astype(jnp.bfloat16).astype(jnp.float32) + got[: chips * tok].reshape(
        chips, tok, part_w
    ).astype(jnp.float32)
    chip_low = low_rows.astype(jnp.float32) + got[chips * tok :].astype(jnp.float32)
    total = lax.dynamic_index_in_dim(chip_sum, chip, 0, keepdims=False)
    total_low = chip_low
    low_send = chip_low.astype(jnp.bfloat16)
    for shift in range(1, chips):
        piece = lax.dynamic_index_in_dim(chip_sum, (chip + shift) % chips, 0, keepdims=False)
        route = [(i, ((i // 2 + shift) % chips) * 2 + i % 2) for i in range(count)]
        sent = jnp.concatenate([piece.astype(jnp.bfloat16), low_send], axis=0)
        recv = lax.ppermute(sent, axis, route).astype(jnp.float32)
        total = total + recv[:tok]
        total_low = total_low + recv[tok:]
    return total, total_low.reshape(low.shape)

def fetch_adapters(stores, req_adapter, holder, wanted, group_id):
    held = stores[0].shape[0]
    total = holder.shape[0]
    names = jnp.arange(total, dtype=jnp.int32)
    used = jnp.any(req_adapter.reshape(-1)[:, None] == names[None, :], axis=0)
    rank = jnp.cumsum(used.astype(jnp.int32)) - 1
    picks = jnp.arange(USED, dtype=jnp.int32)
    hit = used[None, :] & (rank[None, :] == picks[:, None])
    chosen = jnp.sum(jnp.where(hit, names[None, :], 0), axis=1)
    slots = holder[chosen]
    mine = (slots // held) == group_id
    local_idx = slots % held
    flat = jnp.concatenate([s.reshape(held, -1) for s in stores], axis=1)
    compact = jnp.zeros((USED, flat.shape[1]), flat.dtype)
    for h in range(held):
        take_h = (mine & (local_idx == h))[:, None]
        compact = jnp.where(take_h, flat[h][None, :], compact)
    compact = radix_sum(compact, "grp", 4)
    mine_rows = jnp.take(compact, rank[wanted], axis=0)
    out = []
    at = 0
    for s in stores:
        size = math.prod(s.shape[1:])
        out.append(mine_rows[:, at : at + size].reshape((wanted.shape[0],) + s.shape[1:]))
        at += size
    return tuple(out)


def rms_norm(token_rows, norm_gain):
    values = token_rows.astype(jnp.float32)
    norm_scale = lax.rsqrt(jnp.mean(values * values, axis=-1, keepdims=True) + EPSILON)
    return (values * norm_scale * norm_gain).astype(jnp.bfloat16)


def request_layout(lengths, offset, tok_count):
    end_at = jnp.cumsum(lengths)
    starts = end_at - lengths
    row_ids = jnp.arange(tok_count, dtype=jnp.int32)
    segment = jnp.sum((row_ids[:, None] >= end_at[None, :]).astype(jnp.int32), axis=1)
    member = segment[:, None] == jnp.arange(lengths.shape[0], dtype=jnp.int32)[None, :]
    begin_at = jnp.sum(jnp.where(member, starts[None, :], 0), axis=1)
    position = row_ids - begin_at + jnp.where(segment == 0, offset, 0)
    return (segment, member, position)


def rotate(head_rows, position, head_dim):
    half_dim = head_dim // 2
    frequency = THETA ** (-(jnp.arange(half_dim, dtype=jnp.float32) * (2.0 / head_dim)))
    angles = position.astype(jnp.float32)[:, None] * frequency[None, :]
    cosine = jnp.cos(angles)[:, None, :]
    sine_part = jnp.sin(angles)[:, None, :]
    lower_half = head_rows[..., :half_dim]
    upper_half = head_rows[..., half_dim:]
    return jnp.concatenate(
        [
            lower_half * cosine - upper_half * sine_part,
            upper_half * cosine + lower_half * sine_part,
        ],
        axis=-1,
    )


def local(
    tokens,
    norm_gain,
    w_qkv,
    w_out,
    a_in,
    b_in,
    a_out,
    b_out,
    req_len,
    req_adapter,
    holder,
    page_table,
):
    tok_count = tokens.shape[0]
    local_width = w_out.shape[0]
    local_heads = local_width // HD
    req_count = req_len.shape[1]
    rank_dim = a_out.shape[2]
    group_id = lax.axis_index("grp")
    tp_id = lax.axis_index("tp")
    lengths = lax.dynamic_index_in_dim(req_len, group_id, 0, keepdims=False)
    earlier = lax.dynamic_index_in_dim(req_len, jnp.maximum(group_id - 1, 0), 0, keepdims=False)
    continued = group_id > 0
    prev_len = earlier[req_count - 1]
    offset = jnp.where(continued, prev_len, 0)
    segment, member, position = request_layout(lengths, offset, tok_count)
    wanted = lax.dynamic_index_in_dim(req_adapter, group_id, 0, keepdims=False)
    sel_in, sel_up, sel_odown, sel_oup = fetch_adapters(
        (a_in, b_in, a_out, b_out), req_adapter, holder, wanted, group_id
    )
    member_f = member.astype(jnp.float32)
    pick_bf = member.astype(jnp.bfloat16)
    normed = rms_norm(tokens, norm_gain)
    own_cols = lax.dynamic_slice_in_dim(normed, tp_id * local_width, local_width, 1)
    down_f = jnp.einsum("td,rdk->trk", own_cols, sel_in, preferred_element_type=jnp.float32)
    lowrank_f = xor_allreduce(jnp.sum(down_f * member_f[:, :, None], axis=1), "tp")
    lowrank = lowrank_f.astype(jnp.bfloat16)
    spread = (pick_bf[:, :, None] * lowrank[:, None, :]).reshape(tok_count, req_count, 3, rank_dim)
    delta_qkv = jnp.einsum("trck,rckd->tcd", spread, sel_up, preferred_element_type=jnp.float32)
    base_qkv = jnp.dot(
        normed, w_qkv.reshape(w_qkv.shape[0], 3 * local_width), preferred_element_type=jnp.float32
    )
    qkv = (base_qkv.reshape(tok_count, 3, local_width) + delta_qkv).reshape(
        tok_count, 3, local_heads, HD
    )
    query_rows = rotate(qkv[:, 0], position, HD).astype(jnp.bfloat16)
    key_rows = rotate(qkv[:, 1], position, HD).astype(jnp.bfloat16).reshape(tok_count, local_width)
    value_rows = qkv[:, 2].astype(jnp.bfloat16).reshape(tok_count, local_width)
    row_ids = jnp.arange(tok_count, dtype=jnp.int32)
    far_key, far_value = shifted((key_rows, value_rows), "grp", 1)
    far_ok = continued & (segment[:, None] == 0) & (row_ids[None, :] >= tok_count - prev_len)
    far_count = far_key.shape[0]
    near_ok = (segment[:, None] == segment[None, :]) & (row_ids[None, :] <= row_ids[:, None])
    score_scale = 1.0 / math.sqrt(HD)
    far_heads = far_key.reshape(far_count, local_heads, HD)
    near_heads = key_rows.reshape(tok_count, local_heads, HD)
    chunks = 1
    size = tok_count // chunks
    attended_parts = []
    base_parts = []
    for c in range(chunks):
        lo = c * size
        hi = lo + size
        q_c = query_rows[lo:hi]
        near_scores = jnp.einsum(
            "thd,shd->hts", q_c, near_heads[:hi], preferred_element_type=jnp.float32
        )
        far_scores = jnp.einsum(
            "thd,shd->hts", q_c, far_heads, preferred_element_type=jnp.float32
        )
        allowed = jnp.concatenate([far_ok[lo:hi], near_ok[lo:hi, :hi]], axis=1)
        scores = jnp.concatenate([far_scores, near_scores], axis=-1) * score_scale
        scores = jnp.where(allowed[None], scores, -jnp.inf)
        row_top = jnp.max(scores, axis=-1, keepdims=True)
        weights = jnp.exp(scores - row_top)
        weights_bf = (weights / jnp.sum(weights, axis=-1, keepdims=True)).astype(jnp.bfloat16)
        value_c = jnp.concatenate([far_value, value_rows[:hi]], axis=0).reshape(
            far_count + hi, local_heads, HD
        )
        mixed_heads = jnp.einsum(
            "hts,shd->thd", weights_bf, value_c, preferred_element_type=jnp.float32
        )
        attended_c = mixed_heads.astype(jnp.bfloat16).reshape(size, local_width)
        attended_parts.append(attended_c)
    attended = jnp.concatenate(attended_parts, axis=0)
    down_o = jnp.einsum("td,rdk->trk", attended, sel_odown, preferred_element_type=jnp.float32)
    low_part = jnp.sum(down_o * member_f[:, :, None], axis=1).astype(jnp.bfloat16)
    base_out, low_sum = project_scatter(attended, w_out, low_part, "tp")
    low_o = low_sum.astype(jnp.bfloat16)
    spread_o = (pick_bf[:, :, None] * low_o[:, None, :]).reshape(tok_count, req_count * rank_dim)
    delta_o = jnp.dot(
        spread_o,
        sel_oup.reshape(req_count * rank_dim, local_width),
        preferred_element_type=jnp.float32,
    )
    own_rows = lax.dynamic_slice_in_dim(tokens, tp_id * local_width, local_width, 1).astype(
        jnp.float32
    )
    layer_out = (own_rows + base_out + delta_o).astype(jnp.bfloat16)
    page_row = page_table[0]
    page_count = page_row.shape[0]
    numbers = jnp.arange(page_count, dtype=jnp.int32)
    inverse = jnp.sum(jnp.where(page_row[:, None] == numbers[None, :], numbers[:, None], 0), axis=0)
    both_blocks = jnp.stack(
        [
            key_rows.reshape(page_count, PAGE, local_width),
            value_rows.reshape(page_count, PAGE, local_width),
        ],
        axis=1,
    )
    kv_pages = jnp.take(both_blocks, inverse, axis=0)
    return (layer_out, kv_pages)


def solution(mesh):
    return jax.shard_map(
        local,
        mesh=mesh,
        in_specs=(
            P("grp", None),
            P(),
            P(None, None, "tp"),
            P("tp", None),
            P("grp", "tp", None),
            P("grp", None, None, "tp"),
            P("grp", "tp", None),
            P("grp", None, "tp"),
            P(),
            P(),
            P(),
            P("grp", None),
        ),
        out_specs=(P("grp", "tp"), P("grp", None, None, "tp")),
        check_vma=False,
    )
```

```python
import math

import jax
import jax.numpy as jnp
from jax import lax
from jax.sharding import PartitionSpec as P

HD = 128
PAGE = 128


EPSILON = 1e-05
THETA = 10000.0


def shifted(block, axis, distance):
    devices = range(lax.axis_size(axis))
    route = [(i - distance, i) for i in devices if i - distance in devices]
    return lax.ppermute(block, axis, route)


USED = 16


def xor_allreduce(value, axis):
    count = lax.axis_size(axis)
    step = 1
    while step < count:
        route = [(i, i ^ step) for i in range(count)]
        value = value + lax.ppermute(value, axis, route)
        step *= 2
    return value


def xor_halving_sum(buf, axis):
    count = lax.axis_size(axis)
    me = lax.axis_index(axis)
    rows = buf.shape[0]
    cur = buf.reshape((count, -1))
    dists = []
    step = 1
    while step < count:
        dists.append(step)
        step *= 2
    for d in dists:
        bit = (me // d) % 2
        cur = cur.reshape((2, -1) + cur.shape[1:])
        keep = lax.dynamic_index_in_dim(cur, bit, 0, keepdims=False)
        send = lax.dynamic_index_in_dim(cur, 1 - bit, 0, keepdims=False)
        cur = keep + lax.ppermute(send, axis, [(i, i ^ d) for i in range(count)])
    for d in reversed(dists):
        bit = (me // d) % 2
        other = lax.ppermute(cur, axis, [(i, i ^ d) for i in range(count)])
        cur = jnp.where(bit == 0, jnp.stack([cur, other]), jnp.stack([other, cur]))
    return cur.reshape(buf.shape)


def radix_sum(buf, axis, inner):
    count = lax.axis_size(axis)
    outer = count // inner
    me = lax.axis_index(axis)
    lo = me % inner
    hi = me // inner

    def route(shift, size, stride):
        pairs = []
        for i in range(count):
            pos = (i // stride) % size
            pairs.append((i, i + (((pos + shift) % size) - pos) * stride))
        return pairs

    def scatter_step(value, own, size, stride):
        pieces = value.reshape((size, -1) + value.shape[1:])
        total = lax.dynamic_index_in_dim(pieces, own, 0, keepdims=False)
        for shift in range(1, size):
            part = lax.dynamic_index_in_dim(pieces, (own + shift) % size, 0, keepdims=False)
            total = total + lax.ppermute(part, axis, route(shift, size, stride))
        return total

    def gather_step(value, own, size, stride):
        got = [value]
        for shift in range(1, size):
            got.append(lax.ppermute(value, axis, route(shift, size, stride)))
        stack = jnp.stack(got)
        order = (own - jnp.arange(size, dtype=jnp.int32)) % size
        return jnp.take(stack, order, axis=0).reshape((-1,) + value.shape[1:])

    part = scatter_step(buf, lo, inner, 1)
    part = part + lax.ppermute(part, axis, [(i, i ^ inner) for i in range(count)])
    acc = part
    for shift in range(1, outer // 2):
        hop = [(i, (((i // inner) + 2 * shift) % outer) * inner + i % inner) for i in range(count)]
        acc = acc + lax.ppermute(part, axis, hop)
    part = acc
    return gather_step(part, lo, inner, 1)

def project_scatter(attended, w_out, axis):
    count = lax.axis_size(axis)
    me = lax.axis_index(axis)
    core = me % 2
    chip = me // 2
    chips = count // 2
    rows, width = w_out.shape
    part_w = width // count
    w4 = w_out.reshape(rows, chips, 2, part_w)
    w_own = lax.dynamic_index_in_dim(w4, core, 2, keepdims=False)
    w_away = lax.dynamic_index_in_dim(w4, 1 - core, 2, keepdims=False)
    own = jnp.einsum("td,dcw->ctw", attended, w_own, preferred_element_type=jnp.float32)
    away = jnp.einsum("td,dcw->ctw", attended, w_away, preferred_element_type=jnp.float32)
    got = lax.ppermute(away.astype(jnp.bfloat16), axis, [(i, i ^ 1) for i in range(count)])
    chip_sum = own.astype(jnp.bfloat16).astype(jnp.float32) + got.astype(jnp.float32)
    total = lax.dynamic_index_in_dim(chip_sum, chip, 0, keepdims=False)
    for shift in range(1, chips):
        piece = lax.dynamic_index_in_dim(chip_sum, (chip + shift) % chips, 0, keepdims=False)
        route = [(i, ((i // 2 + shift) % chips) * 2 + i % 2) for i in range(count)]
        total = total + lax.ppermute(piece.astype(jnp.bfloat16), axis, route).astype(jnp.float32)
    return total


def fetch_adapters(stores, req_adapter, holder, wanted, group_id):
    held = stores[0].shape[0]
    total = holder.shape[0]
    names = jnp.arange(total, dtype=jnp.int32)
    used = jnp.any(req_adapter.reshape(-1)[:, None] == names[None, :], axis=0)
    rank = jnp.cumsum(used.astype(jnp.int32)) - 1
    picks = jnp.arange(USED, dtype=jnp.int32)
    hit = used[None, :] & (rank[None, :] == picks[:, None])
    chosen = jnp.sum(jnp.where(hit, names[None, :], 0), axis=1)
    slots = holder[chosen]
    mine = (slots // held) == group_id
    local_idx = slots % held
    flat = jnp.concatenate([s.reshape(held, -1) for s in stores], axis=1)
    compact = jnp.zeros((USED, flat.shape[1]), flat.dtype)
    for h in range(held):
        take_h = (mine & (local_idx == h))[:, None]
        compact = jnp.where(take_h, flat[h][None, :], compact)
    compact = radix_sum(compact, "grp", 4)
    mine_rows = jnp.take(compact, rank[wanted], axis=0)
    out = []
    at = 0
    for s in stores:
        size = math.prod(s.shape[1:])
        out.append(mine_rows[:, at : at + size].reshape((wanted.shape[0],) + s.shape[1:]))
        at += size
    return tuple(out)


def rms_norm(token_rows, norm_gain):
    values = token_rows.astype(jnp.float32)
    norm_scale = lax.rsqrt(jnp.mean(values * values, axis=-1, keepdims=True) + EPSILON)
    return (values * norm_scale * norm_gain).astype(jnp.bfloat16)


def request_layout(lengths, offset, tok_count):
    end_at = jnp.cumsum(lengths)
    starts = end_at - lengths
    row_ids = jnp.arange(tok_count, dtype=jnp.int32)
    segment = jnp.sum((row_ids[:, None] >= end_at[None, :]).astype(jnp.int32), axis=1)
    member = segment[:, None] == jnp.arange(lengths.shape[0], dtype=jnp.int32)[None, :]
    begin_at = jnp.sum(jnp.where(member, starts[None, :], 0), axis=1)
    position = row_ids - begin_at + jnp.where(segment == 0, offset, 0)
    return (segment, member, position)


def rotate(head_rows, position, head_dim):
    half_dim = head_dim // 2
    frequency = THETA ** (-(jnp.arange(half_dim, dtype=jnp.float32) * (2.0 / head_dim)))
    angles = position.astype(jnp.float32)[:, None] * frequency[None, :]
    cosine = jnp.cos(angles)[:, None, :]
    sine_part = jnp.sin(angles)[:, None, :]
    lower_half = head_rows[..., :half_dim]
    upper_half = head_rows[..., half_dim:]
    return jnp.concatenate(
        [
            lower_half * cosine - upper_half * sine_part,
            upper_half * cosine + lower_half * sine_part,
        ],
        axis=-1,
    )


def local(
    tokens,
    norm_gain,
    w_qkv,
    w_out,
    a_in,
    b_in,
    a_out,
    b_out,
    req_len,
    req_adapter,
    holder,
    page_table,
):
    tok_count = tokens.shape[0]
    local_width = w_out.shape[0]
    local_heads = local_width // HD
    req_count = req_len.shape[1]
    rank_dim = a_out.shape[2]
    group_id = lax.axis_index("grp")
    tp_id = lax.axis_index("tp")
    lengths = lax.dynamic_index_in_dim(req_len, group_id, 0, keepdims=False)
    earlier = lax.dynamic_index_in_dim(req_len, jnp.maximum(group_id - 1, 0), 0, keepdims=False)
    continued = group_id > 0
    prev_len = earlier[req_count - 1]
    offset = jnp.where(continued, prev_len, 0)
    segment, member, position = request_layout(lengths, offset, tok_count)
    wanted = lax.dynamic_index_in_dim(req_adapter, group_id, 0, keepdims=False)
    sel_in, sel_up, sel_odown, sel_oup = fetch_adapters(
        (a_in, b_in, a_out, b_out), req_adapter, holder, wanted, group_id
    )
    member_f = member.astype(jnp.float32)
    pick_bf = member.astype(jnp.bfloat16)
    normed = rms_norm(tokens, norm_gain)
    own_cols = lax.dynamic_slice_in_dim(normed, tp_id * local_width, local_width, 1)
    down_f = jnp.einsum("td,rdk->trk", own_cols, sel_in, preferred_element_type=jnp.float32)
    lowrank_f = xor_allreduce(jnp.sum(down_f * member_f[:, :, None], axis=1), "tp")
    lowrank = lowrank_f.astype(jnp.bfloat16)
    spread = (pick_bf[:, :, None] * lowrank[:, None, :]).reshape(tok_count, req_count, 3, rank_dim)
    delta_qkv = jnp.einsum("trck,rckd->tcd", spread, sel_up, preferred_element_type=jnp.float32)
    base_qkv = jnp.dot(
        normed, w_qkv.reshape(w_qkv.shape[0], 3 * local_width), preferred_element_type=jnp.float32
    )
    qkv = (base_qkv.reshape(tok_count, 3, local_width) + delta_qkv).reshape(
        tok_count, 3, local_heads, HD
    )
    query_rows = rotate(qkv[:, 0], position, HD).astype(jnp.bfloat16)
    key_rows = rotate(qkv[:, 1], position, HD).astype(jnp.bfloat16).reshape(tok_count, local_width)
    value_rows = qkv[:, 2].astype(jnp.bfloat16).reshape(tok_count, local_width)
    row_ids = jnp.arange(tok_count, dtype=jnp.int32)
    far_key, far_value = shifted((key_rows, value_rows), "grp", 1)
    far_ok = continued & (segment[:, None] == 0) & (row_ids[None, :] >= tok_count - prev_len)
    far_count = far_key.shape[0]
    near_ok = (segment[:, None] == segment[None, :]) & (row_ids[None, :] <= row_ids[:, None])
    score_scale = 1.0 / math.sqrt(HD)
    far_heads = far_key.reshape(far_count, local_heads, HD)
    near_heads = key_rows.reshape(tok_count, local_heads, HD)
    chunks = 1
    size = tok_count // chunks
    attended_parts = []
    base_parts = []
    for c in range(chunks):
        lo = c * size
        hi = lo + size
        q_c = query_rows[lo:hi]
        near_scores = jnp.einsum(
            "thd,shd->hts", q_c, near_heads[:hi], preferred_element_type=jnp.float32
        )
        far_scores = jnp.einsum(
            "thd,shd->hts", q_c, far_heads, preferred_element_type=jnp.float32
        )
        allowed = jnp.concatenate([far_ok[lo:hi], near_ok[lo:hi, :hi]], axis=1)
        scores = jnp.concatenate([far_scores, near_scores], axis=-1) * score_scale
        scores = jnp.where(allowed[None], scores, -jnp.inf)
        row_top = jnp.max(scores, axis=-1, keepdims=True)
        weights = jnp.exp(scores - row_top)
        weights_bf = (weights / jnp.sum(weights, axis=-1, keepdims=True)).astype(jnp.bfloat16)
        value_c = jnp.concatenate([far_value, value_rows[:hi]], axis=0).reshape(
            far_count + hi, local_heads, HD
        )
        mixed_heads = jnp.einsum(
            "hts,shd->thd", weights_bf, value_c, preferred_element_type=jnp.float32
        )
        attended_c = mixed_heads.astype(jnp.bfloat16).reshape(size, local_width)
        base_parts.append(project_scatter(attended_c, w_out, "tp"))
        attended_parts.append(attended_c)
    attended = jnp.concatenate(attended_parts, axis=0)
    base_out = jnp.concatenate(base_parts, axis=0)
    down_o = jnp.einsum("td,rdk->trk", attended, sel_odown, preferred_element_type=jnp.float32)
    low_part = jnp.sum(down_o * member_f[:, :, None], axis=1).astype(jnp.bfloat16)
    low_o = xor_allreduce(low_part, "tp")
    spread_o = (pick_bf[:, :, None] * low_o[:, None, :]).reshape(tok_count, req_count * rank_dim)
    delta_o = jnp.dot(
        spread_o,
        sel_oup.reshape(req_count * rank_dim, local_width),
        preferred_element_type=jnp.float32,
    )
    own_rows = lax.dynamic_slice_in_dim(tokens, tp_id * local_width, local_width, 1).astype(
        jnp.float32
    )
    layer_out = (own_rows + base_out + delta_o).astype(jnp.bfloat16)
    page_row = page_table[0]
    page_count = page_row.shape[0]
    numbers = jnp.arange(page_count, dtype=jnp.int32)
    inverse = jnp.sum(jnp.where(page_row[:, None] == numbers[None, :], numbers[:, None], 0), axis=0)
    both_blocks = jnp.stack(
        [
            key_rows.reshape(page_count, PAGE, local_width),
            value_rows.reshape(page_count, PAGE, local_width),
        ],
        axis=1,
    )
    kv_pages = jnp.take(both_blocks, inverse, axis=0)
    return (layer_out, kv_pages)


def solution(mesh):
    return jax.shard_map(
        local,
        mesh=mesh,
        in_specs=(
            P("grp", None),
            P(),
            P(None, None, "tp"),
            P("tp", None),
            P("grp", "tp", None),
            P("grp", None, None, "tp"),
            P("grp", "tp", None),
            P("grp", None, "tp"),
            P(),
            P(),
            P(),
            P("grp", None),
        ),
        out_specs=(P("grp", "tp"), P("grp", None, None, "tp")),
        check_vma=False,
    )
```

```python
import math

import jax
import jax.numpy as jnp
from jax import lax
from jax.sharding import PartitionSpec as P

HD = 128
PAGE = 128


EPSILON = 1e-05
THETA = 10000.0


def shifted(block, axis, distance):
    devices = range(lax.axis_size(axis))
    route = [(i - distance, i) for i in devices if i - distance in devices]
    return lax.ppermute(block, axis, route)


USED = 16


def xor_allreduce(value, axis):
    count = lax.axis_size(axis)
    step = 1
    while step < count:
        route = [(i, i ^ step) for i in range(count)]
        value = value + lax.ppermute(value, axis, route)
        step *= 2
    return value


def xor_halving_sum(buf, axis):
    count = lax.axis_size(axis)
    me = lax.axis_index(axis)
    rows = buf.shape[0]
    cur = buf.reshape((count, -1))
    dists = []
    step = 1
    while step < count:
        dists.append(step)
        step *= 2
    for d in dists:
        bit = (me // d) % 2
        cur = cur.reshape((2, -1) + cur.shape[1:])
        keep = lax.dynamic_index_in_dim(cur, bit, 0, keepdims=False)
        send = lax.dynamic_index_in_dim(cur, 1 - bit, 0, keepdims=False)
        cur = keep + lax.ppermute(send, axis, [(i, i ^ d) for i in range(count)])
    for d in reversed(dists):
        bit = (me // d) % 2
        other = lax.ppermute(cur, axis, [(i, i ^ d) for i in range(count)])
        cur = jnp.where(bit == 0, jnp.stack([cur, other]), jnp.stack([other, cur]))
    return cur.reshape(buf.shape)


def radix_sum(buf, axis, inner):
    count = lax.axis_size(axis)
    outer = count // inner
    me = lax.axis_index(axis)
    lo = me % inner
    hi = me // inner

    def route(shift, size, stride):
        pairs = []
        for i in range(count):
            pos = (i // stride) % size
            pairs.append((i, i + (((pos + shift) % size) - pos) * stride))
        return pairs

    def scatter_step(value, own, size, stride):
        pieces = value.reshape((size, -1) + value.shape[1:])
        total = lax.dynamic_index_in_dim(pieces, own, 0, keepdims=False)
        for shift in range(1, size):
            part = lax.dynamic_index_in_dim(pieces, (own + shift) % size, 0, keepdims=False)
            total = total + lax.ppermute(part, axis, route(shift, size, stride))
        return total

    def gather_step(value, own, size, stride):
        got = [value]
        for shift in range(1, size):
            got.append(lax.ppermute(value, axis, route(shift, size, stride)))
        stack = jnp.stack(got)
        order = (own - jnp.arange(size, dtype=jnp.int32)) % size
        return jnp.take(stack, order, axis=0).reshape((-1,) + value.shape[1:])

    part = scatter_step(buf, lo, inner, 1)
    step = inner
    while step < count:
        part = part + lax.ppermute(part, axis, [(i, i ^ step) for i in range(count)])
        step *= 2
    return gather_step(part, lo, inner, 1)

def project_scatter(attended, w_out, axis):
    count = lax.axis_size(axis)
    me = lax.axis_index(axis)
    core = me % 2
    chip = me // 2
    chips = count // 2
    rows, width = w_out.shape
    part_w = width // count
    w4 = w_out.reshape(rows, chips, 2, part_w)
    w_own = lax.dynamic_index_in_dim(w4, core, 2, keepdims=False)
    w_away = lax.dynamic_index_in_dim(w4, 1 - core, 2, keepdims=False)
    own = jnp.einsum("td,dcw->ctw", attended, w_own, preferred_element_type=jnp.float32)
    away = jnp.einsum("td,dcw->ctw", attended, w_away, preferred_element_type=jnp.float32)
    got = lax.ppermute(away.astype(jnp.bfloat16), axis, [(i, i ^ 1) for i in range(count)])
    chip_sum = own.astype(jnp.bfloat16).astype(jnp.float32) + got.astype(jnp.float32)
    total = lax.dynamic_index_in_dim(chip_sum, chip, 0, keepdims=False)
    for shift in range(1, chips):
        piece = lax.dynamic_index_in_dim(chip_sum, (chip + shift) % chips, 0, keepdims=False)
        route = [(i, ((i // 2 + shift) % chips) * 2 + i % 2) for i in range(count)]
        total = total + lax.ppermute(piece.astype(jnp.bfloat16), axis, route).astype(jnp.float32)
    return total


def pair_allreduce(value, axis):
    count = lax.axis_size(axis)
    chips = count // 2
    value = value + lax.ppermute(value, axis, [(i, i ^ 1) for i in range(count)])
    total = value
    for shift in range(1, chips):
        route = [(i, ((i // 2 + shift) % chips) * 2 + i % 2) for i in range(count)]
        total = total + lax.ppermute(value, axis, route)
    return total


def fetch_adapters(stores, req_adapter, holder, wanted, group_id):
    held = stores[0].shape[0]
    total = holder.shape[0]
    names = jnp.arange(total, dtype=jnp.int32)
    used = jnp.any(req_adapter.reshape(-1)[:, None] == names[None, :], axis=0)
    rank = jnp.cumsum(used.astype(jnp.int32)) - 1
    picks = jnp.arange(USED, dtype=jnp.int32)
    hit = used[None, :] & (rank[None, :] == picks[:, None])
    chosen = jnp.sum(jnp.where(hit, names[None, :], 0), axis=1)
    slots = holder[chosen]
    mine = (slots // held) == group_id
    local_idx = slots % held
    flat = jnp.concatenate([s.reshape(held, -1) for s in stores], axis=1)
    compact = jnp.zeros((USED, flat.shape[1]), flat.dtype)
    for h in range(held):
        take_h = (mine & (local_idx == h))[:, None]
        compact = jnp.where(take_h, flat[h][None, :], compact)
    compact = radix_sum(compact, "grp", 4)
    mine_rows = jnp.take(compact, rank[wanted], axis=0)
    out = []
    at = 0
    for s in stores:
        size = math.prod(s.shape[1:])
        out.append(mine_rows[:, at : at + size].reshape((wanted.shape[0],) + s.shape[1:]))
        at += size
    return tuple(out)


def rms_norm(token_rows, norm_gain):
    values = token_rows.astype(jnp.float32)
    norm_scale = lax.rsqrt(jnp.mean(values * values, axis=-1, keepdims=True) + EPSILON)
    return (values * norm_scale * norm_gain).astype(jnp.bfloat16)


def request_layout(lengths, offset, tok_count):
    end_at = jnp.cumsum(lengths)
    starts = end_at - lengths
    row_ids = jnp.arange(tok_count, dtype=jnp.int32)
    segment = jnp.sum((row_ids[:, None] >= end_at[None, :]).astype(jnp.int32), axis=1)
    member = segment[:, None] == jnp.arange(lengths.shape[0], dtype=jnp.int32)[None, :]
    begin_at = jnp.sum(jnp.where(member, starts[None, :], 0), axis=1)
    position = row_ids - begin_at + jnp.where(segment == 0, offset, 0)
    return (segment, member, position)


def rotate(head_rows, position, head_dim):
    half_dim = head_dim // 2
    frequency = THETA ** (-(jnp.arange(half_dim, dtype=jnp.float32) * (2.0 / head_dim)))
    angles = position.astype(jnp.float32)[:, None] * frequency[None, :]
    cosine = jnp.cos(angles)[:, None, :]
    sine_part = jnp.sin(angles)[:, None, :]
    lower_half = head_rows[..., :half_dim]
    upper_half = head_rows[..., half_dim:]
    return jnp.concatenate(
        [
            lower_half * cosine - upper_half * sine_part,
            upper_half * cosine + lower_half * sine_part,
        ],
        axis=-1,
    )


def local(
    tokens,
    norm_gain,
    w_qkv,
    w_out,
    a_in,
    b_in,
    a_out,
    b_out,
    req_len,
    req_adapter,
    holder,
    page_table,
):
    tok_count = tokens.shape[0]
    local_width = w_out.shape[0]
    local_heads = local_width // HD
    req_count = req_len.shape[1]
    rank_dim = a_out.shape[2]
    group_id = lax.axis_index("grp")
    tp_id = lax.axis_index("tp")
    lengths = lax.dynamic_index_in_dim(req_len, group_id, 0, keepdims=False)
    earlier = lax.dynamic_index_in_dim(req_len, jnp.maximum(group_id - 1, 0), 0, keepdims=False)
    continued = group_id > 0
    prev_len = earlier[req_count - 1]
    offset = jnp.where(continued, prev_len, 0)
    segment, member, position = request_layout(lengths, offset, tok_count)
    wanted = lax.dynamic_index_in_dim(req_adapter, group_id, 0, keepdims=False)
    sel_in, sel_up, sel_odown, sel_oup = fetch_adapters(
        (a_in, b_in, a_out, b_out), req_adapter, holder, wanted, group_id
    )
    member_f = member.astype(jnp.float32)
    pick_bf = member.astype(jnp.bfloat16)
    normed = rms_norm(tokens, norm_gain)
    own_cols = lax.dynamic_slice_in_dim(normed, tp_id * local_width, local_width, 1)
    down_f = jnp.einsum("td,rdk->trk", own_cols, sel_in, preferred_element_type=jnp.float32)
    lowrank_f = pair_allreduce(jnp.sum(down_f * member_f[:, :, None], axis=1), "tp")
    lowrank = lowrank_f.astype(jnp.bfloat16)
    spread = (pick_bf[:, :, None] * lowrank[:, None, :]).reshape(tok_count, req_count, 3, rank_dim)
    delta_qkv = jnp.einsum("trck,rckd->tcd", spread, sel_up, preferred_element_type=jnp.float32)
    base_qkv = jnp.dot(
        normed, w_qkv.reshape(w_qkv.shape[0], 3 * local_width), preferred_element_type=jnp.float32
    )
    qkv = (base_qkv.reshape(tok_count, 3, local_width) + delta_qkv).reshape(
        tok_count, 3, local_heads, HD
    )
    query_rows = rotate(qkv[:, 0], position, HD).astype(jnp.bfloat16)
    key_rows = rotate(qkv[:, 1], position, HD).astype(jnp.bfloat16).reshape(tok_count, local_width)
    value_rows = qkv[:, 2].astype(jnp.bfloat16).reshape(tok_count, local_width)
    row_ids = jnp.arange(tok_count, dtype=jnp.int32)
    far_key, far_value = shifted((key_rows, value_rows), "grp", 1)
    far_ok = continued & (segment[:, None] == 0) & (row_ids[None, :] >= tok_count - prev_len)
    far_count = far_key.shape[0]
    near_ok = (segment[:, None] == segment[None, :]) & (row_ids[None, :] <= row_ids[:, None])
    score_scale = 1.0 / math.sqrt(HD)
    far_heads = far_key.reshape(far_count, local_heads, HD)
    near_heads = key_rows.reshape(tok_count, local_heads, HD)
    chunks = 1
    size = tok_count // chunks
    attended_parts = []
    base_parts = []
    for c in range(chunks):
        lo = c * size
        hi = lo + size
        q_c = query_rows[lo:hi]
        near_scores = jnp.einsum(
            "thd,shd->hts", q_c, near_heads[:hi], preferred_element_type=jnp.float32
        )
        far_scores = jnp.einsum(
            "thd,shd->hts", q_c, far_heads, preferred_element_type=jnp.float32
        )
        allowed = jnp.concatenate([far_ok[lo:hi], near_ok[lo:hi, :hi]], axis=1)
        scores = jnp.concatenate([far_scores, near_scores], axis=-1) * score_scale
        scores = jnp.where(allowed[None], scores, -jnp.inf)
        row_top = jnp.max(scores, axis=-1, keepdims=True)
        weights = jnp.exp(scores - row_top)
        weights_bf = (weights / jnp.sum(weights, axis=-1, keepdims=True)).astype(jnp.bfloat16)
        value_c = jnp.concatenate([far_value, value_rows[:hi]], axis=0).reshape(
            far_count + hi, local_heads, HD
        )
        mixed_heads = jnp.einsum(
            "hts,shd->thd", weights_bf, value_c, preferred_element_type=jnp.float32
        )
        attended_c = mixed_heads.astype(jnp.bfloat16).reshape(size, local_width)
        base_parts.append(project_scatter(attended_c, w_out, "tp"))
        attended_parts.append(attended_c)
    attended = jnp.concatenate(attended_parts, axis=0)
    base_out = jnp.concatenate(base_parts, axis=0)
    down_o = jnp.einsum("td,rdk->trk", attended, sel_odown, preferred_element_type=jnp.float32)
    low_part = jnp.sum(down_o * member_f[:, :, None], axis=1).astype(jnp.bfloat16)
    low_o = xor_allreduce(low_part, "tp")
    spread_o = (pick_bf[:, :, None] * low_o[:, None, :]).reshape(tok_count, req_count * rank_dim)
    delta_o = jnp.dot(
        spread_o,
        sel_oup.reshape(req_count * rank_dim, local_width),
        preferred_element_type=jnp.float32,
    )
    own_rows = lax.dynamic_slice_in_dim(tokens, tp_id * local_width, local_width, 1).astype(
        jnp.float32
    )
    layer_out = (own_rows + base_out + delta_o).astype(jnp.bfloat16)
    page_row = page_table[0]
    page_count = page_row.shape[0]
    numbers = jnp.arange(page_count, dtype=jnp.int32)
    inverse = jnp.sum(jnp.where(page_row[:, None] == numbers[None, :], numbers[:, None], 0), axis=0)
    both_blocks = jnp.stack(
        [
            key_rows.reshape(page_count, PAGE, local_width),
            value_rows.reshape(page_count, PAGE, local_width),
        ],
        axis=1,
    )
    kv_pages = jnp.take(both_blocks, inverse, axis=0)
    return (layer_out, kv_pages)


def solution(mesh):
    return jax.shard_map(
        local,
        mesh=mesh,
        in_specs=(
            P("grp", None),
            P(),
            P(None, None, "tp"),
            P("tp", None),
            P("grp", "tp", None),
            P("grp", None, None, "tp"),
            P("grp", "tp", None),
            P("grp", None, "tp"),
            P(),
            P(),
            P(),
            P("grp", None),
        ),
        out_specs=(P("grp", "tp"), P("grp", None, None, "tp")),
        check_vma=False,
    )
```

```python
import math

import jax
import jax.numpy as jnp
from jax import lax
from jax.sharding import PartitionSpec as P

HD = 128
PAGE = 128


EPSILON = 1e-05
THETA = 10000.0


def shifted(block, axis, distance):
    devices = range(lax.axis_size(axis))
    route = [(i - distance, i) for i in devices if i - distance in devices]
    return lax.ppermute(block, axis, route)


USED = 16


def xor_allreduce(value, axis):
    count = lax.axis_size(axis)
    step = 1
    while step < count:
        route = [(i, i ^ step) for i in range(count)]
        value = value + lax.ppermute(value, axis, route)
        step *= 2
    return value


def xor_halving_sum(buf, axis):
    count = lax.axis_size(axis)
    me = lax.axis_index(axis)
    rows = buf.shape[0]
    cur = buf.reshape((count, -1))
    dists = []
    step = 1
    while step < count:
        dists.append(step)
        step *= 2
    for d in dists:
        bit = (me // d) % 2
        cur = cur.reshape((2, -1) + cur.shape[1:])
        keep = lax.dynamic_index_in_dim(cur, bit, 0, keepdims=False)
        send = lax.dynamic_index_in_dim(cur, 1 - bit, 0, keepdims=False)
        cur = keep + lax.ppermute(send, axis, [(i, i ^ d) for i in range(count)])
    for d in reversed(dists):
        bit = (me // d) % 2
        other = lax.ppermute(cur, axis, [(i, i ^ d) for i in range(count)])
        cur = jnp.where(bit == 0, jnp.stack([cur, other]), jnp.stack([other, cur]))
    return cur.reshape(buf.shape)


def radix_sum(buf, axis, inner):
    count = lax.axis_size(axis)
    outer = count // inner
    me = lax.axis_index(axis)
    lo = me % inner
    hi = me // inner

    def route(shift, size, stride):
        pairs = []
        for i in range(count):
            pos = (i // stride) % size
            pairs.append((i, i + (((pos + shift) % size) - pos) * stride))
        return pairs

    def scatter_step(value, own, size, stride):
        pieces = value.reshape((size, -1) + value.shape[1:])
        total = lax.dynamic_index_in_dim(pieces, own, 0, keepdims=False)
        for shift in range(1, size):
            part = lax.dynamic_index_in_dim(pieces, (own + shift) % size, 0, keepdims=False)
            total = total + lax.ppermute(part, axis, route(shift, size, stride))
        return total

    def gather_step(value, own, size, stride):
        got = [value]
        for shift in range(1, size):
            got.append(lax.ppermute(value, axis, route(shift, size, stride)))
        stack = jnp.stack(got)
        order = (own - jnp.arange(size, dtype=jnp.int32)) % size
        return jnp.take(stack, order, axis=0).reshape((-1,) + value.shape[1:])

    part = scatter_step(buf, lo, inner, 1)
    step = inner
    while step < count:
        part = part + lax.ppermute(part, axis, [(i, i ^ step) for i in range(count)])
        step *= 2
    return gather_step(part, lo, inner, 1)

def project_scatter(attended, w_out, axis):
    count = lax.axis_size(axis)
    me = lax.axis_index(axis)
    core = me % 2
    chip = me // 2
    chips = count // 2
    rows, width = w_out.shape
    part_w = width // count
    w4 = w_out.reshape(rows, chips, 2, part_w)
    w_own = lax.dynamic_index_in_dim(w4, core, 2, keepdims=False)
    w_away = lax.dynamic_index_in_dim(w4, 1 - core, 2, keepdims=False)
    own = jnp.einsum("td,dcw->ctw", attended, w_own, preferred_element_type=jnp.float32)
    away = jnp.einsum("td,dcw->ctw", attended, w_away, preferred_element_type=jnp.float32)
    got = lax.ppermute(away.astype(jnp.bfloat16), axis, [(i, i ^ 1) for i in range(count)])
    chip_sum = own.astype(jnp.bfloat16).astype(jnp.float32) + got.astype(jnp.float32)
    total = lax.dynamic_index_in_dim(chip_sum, chip, 0, keepdims=False)
    for shift in range(1, chips):
        piece = lax.dynamic_index_in_dim(chip_sum, (chip + shift) % chips, 0, keepdims=False)
        route = [(i, ((i // 2 + shift) % chips) * 2 + i % 2) for i in range(count)]
        total = total + lax.ppermute(piece.astype(jnp.bfloat16), axis, route).astype(jnp.float32)
    return total


def pair_allreduce(value, axis):
    count = lax.axis_size(axis)
    chips = count // 2
    value = value + lax.ppermute(value, axis, [(i, i ^ 1) for i in range(count)])
    total = value
    for shift in range(1, chips):
        route = [(i, ((i // 2 + shift) % chips) * 2 + i % 2) for i in range(count)]
        total = total + lax.ppermute(value, axis, route)
    return total


def fetch_adapters(stores, req_adapter, holder, wanted, group_id):
    held = stores[0].shape[0]
    total = holder.shape[0]
    names = jnp.arange(total, dtype=jnp.int32)
    used = jnp.any(req_adapter.reshape(-1)[:, None] == names[None, :], axis=0)
    rank = jnp.cumsum(used.astype(jnp.int32)) - 1
    picks = jnp.arange(USED, dtype=jnp.int32)
    hit = used[None, :] & (rank[None, :] == picks[:, None])
    chosen = jnp.sum(jnp.where(hit, names[None, :], 0), axis=1)
    slots = holder[chosen]
    mine = (slots // held) == group_id
    local_idx = slots % held
    flat = jnp.concatenate([s.reshape(held, -1) for s in stores], axis=1)
    compact = jnp.zeros((USED, flat.shape[1]), flat.dtype)
    for h in range(held):
        take_h = (mine & (local_idx == h))[:, None]
        compact = jnp.where(take_h, flat[h][None, :], compact)
    compact = radix_sum(compact, "grp", 4)
    mine_rows = jnp.take(compact, rank[wanted], axis=0)
    out = []
    at = 0
    for s in stores:
        size = math.prod(s.shape[1:])
        out.append(mine_rows[:, at : at + size].reshape((wanted.shape[0],) + s.shape[1:]))
        at += size
    return tuple(out)


def rms_norm(token_rows, norm_gain):
    values = token_rows.astype(jnp.float32)
    norm_scale = lax.rsqrt(jnp.mean(values * values, axis=-1, keepdims=True) + EPSILON)
    return (values * norm_scale * norm_gain).astype(jnp.bfloat16)


def request_layout(lengths, offset, tok_count):
    end_at = jnp.cumsum(lengths)
    starts = end_at - lengths
    row_ids = jnp.arange(tok_count, dtype=jnp.int32)
    segment = jnp.sum((row_ids[:, None] >= end_at[None, :]).astype(jnp.int32), axis=1)
    member = segment[:, None] == jnp.arange(lengths.shape[0], dtype=jnp.int32)[None, :]
    begin_at = jnp.sum(jnp.where(member, starts[None, :], 0), axis=1)
    position = row_ids - begin_at + jnp.where(segment == 0, offset, 0)
    return (segment, member, position)


def rotate(head_rows, position, head_dim):
    half_dim = head_dim // 2
    frequency = THETA ** (-(jnp.arange(half_dim, dtype=jnp.float32) * (2.0 / head_dim)))
    angles = position.astype(jnp.float32)[:, None] * frequency[None, :]
    cosine = jnp.cos(angles)[:, None, :]
    sine_part = jnp.sin(angles)[:, None, :]
    lower_half = head_rows[..., :half_dim]
    upper_half = head_rows[..., half_dim:]
    return jnp.concatenate(
        [
            lower_half * cosine - upper_half * sine_part,
            upper_half * cosine + lower_half * sine_part,
        ],
        axis=-1,
    )


def local(
    tokens,
    norm_gain,
    w_qkv,
    w_out,
    a_in,
    b_in,
    a_out,
    b_out,
    req_len,
    req_adapter,
    holder,
    page_table,
):
    tok_count = tokens.shape[0]
    local_width = w_out.shape[0]
    local_heads = local_width // HD
    req_count = req_len.shape[1]
    rank_dim = a_out.shape[2]
    group_id = lax.axis_index("grp")
    tp_id = lax.axis_index("tp")
    lengths = lax.dynamic_index_in_dim(req_len, group_id, 0, keepdims=False)
    earlier = lax.dynamic_index_in_dim(req_len, jnp.maximum(group_id - 1, 0), 0, keepdims=False)
    continued = group_id > 0
    prev_len = earlier[req_count - 1]
    offset = jnp.where(continued, prev_len, 0)
    segment, member, position = request_layout(lengths, offset, tok_count)
    wanted = lax.dynamic_index_in_dim(req_adapter, group_id, 0, keepdims=False)
    sel_in, sel_up, sel_odown, sel_oup = fetch_adapters(
        (a_in, b_in, a_out, b_out), req_adapter, holder, wanted, group_id
    )
    member_f = member.astype(jnp.float32)
    pick_bf = member.astype(jnp.bfloat16)
    normed = rms_norm(tokens, norm_gain)
    own_cols = lax.dynamic_slice_in_dim(normed, tp_id * local_width, local_width, 1)
    down_f = jnp.einsum("td,rdk->trk", own_cols, sel_in, preferred_element_type=jnp.float32)
    lowrank_f = pair_allreduce(jnp.sum(down_f * member_f[:, :, None], axis=1), "tp")
    lowrank = lowrank_f.astype(jnp.bfloat16)
    spread = (pick_bf[:, :, None] * lowrank[:, None, :]).reshape(tok_count, req_count, 3, rank_dim)
    delta_qkv = jnp.einsum("trck,rckd->tcd", spread, sel_up, preferred_element_type=jnp.float32)
    base_qkv = jnp.dot(
        normed, w_qkv.reshape(w_qkv.shape[0], 3 * local_width), preferred_element_type=jnp.float32
    )
    qkv = (base_qkv.reshape(tok_count, 3, local_width) + delta_qkv).reshape(
        tok_count, 3, local_heads, HD
    )
    query_rows = rotate(qkv[:, 0], position, HD).astype(jnp.bfloat16)
    key_rows = rotate(qkv[:, 1], position, HD).astype(jnp.bfloat16).reshape(tok_count, local_width)
    value_rows = qkv[:, 2].astype(jnp.bfloat16).reshape(tok_count, local_width)
    row_ids = jnp.arange(tok_count, dtype=jnp.int32)
    far_key, far_value = shifted((key_rows, value_rows), "grp", 1)
    far_ok = continued & (segment[:, None] == 0) & (row_ids[None, :] >= tok_count - prev_len)
    far_count = far_key.shape[0]
    near_ok = (segment[:, None] == segment[None, :]) & (row_ids[None, :] <= row_ids[:, None])
    score_scale = 1.0 / math.sqrt(HD)
    far_heads = far_key.reshape(far_count, local_heads, HD)
    near_heads = key_rows.reshape(tok_count, local_heads, HD)
    chunks = 1
    size = tok_count // chunks
    attended_parts = []
    base_parts = []
    for c in range(chunks):
        lo = c * size
        hi = lo + size
        q_c = query_rows[lo:hi]
        near_scores = jnp.einsum(
            "thd,shd->hts", q_c, near_heads[:hi], preferred_element_type=jnp.float32
        )
        far_scores = jnp.einsum(
            "thd,shd->hts", q_c, far_heads, preferred_element_type=jnp.float32
        )
        allowed = jnp.concatenate([far_ok[lo:hi], near_ok[lo:hi, :hi]], axis=1)
        scores = jnp.concatenate([far_scores, near_scores], axis=-1) * score_scale
        scores = jnp.where(allowed[None], scores, -jnp.inf)
        row_top = jnp.max(scores, axis=-1, keepdims=True)
        weights = jnp.exp(scores - row_top)
        weights_bf = (weights / jnp.sum(weights, axis=-1, keepdims=True)).astype(jnp.bfloat16)
        value_c = jnp.concatenate([far_value, value_rows[:hi]], axis=0).reshape(
            far_count + hi, local_heads, HD
        )
        mixed_heads = jnp.einsum(
            "hts,shd->thd", weights_bf, value_c, preferred_element_type=jnp.float32
        )
        attended_c = mixed_heads.astype(jnp.bfloat16).reshape(size, local_width)
        base_parts.append(project_scatter(attended_c, w_out, "tp"))
        attended_parts.append(attended_c)
    attended = jnp.concatenate(attended_parts, axis=0)
    base_out = jnp.concatenate(base_parts, axis=0)
    down_o = jnp.einsum("td,rdk->trk", attended, sel_odown, preferred_element_type=jnp.float32)
    low_part = jnp.sum(down_o * member_f[:, :, None], axis=1).astype(jnp.bfloat16)
    low_o = pair_allreduce(low_part, "tp")
    spread_o = (pick_bf[:, :, None] * low_o[:, None, :]).reshape(tok_count, req_count * rank_dim)
    delta_o = jnp.dot(
        spread_o,
        sel_oup.reshape(req_count * rank_dim, local_width),
        preferred_element_type=jnp.float32,
    )
    own_rows = lax.dynamic_slice_in_dim(tokens, tp_id * local_width, local_width, 1).astype(
        jnp.float32
    )
    layer_out = (own_rows + base_out + delta_o).astype(jnp.bfloat16)
    page_row = page_table[0]
    page_count = page_row.shape[0]
    numbers = jnp.arange(page_count, dtype=jnp.int32)
    inverse = jnp.sum(jnp.where(page_row[:, None] == numbers[None, :], numbers[:, None], 0), axis=0)
    both_blocks = jnp.stack(
        [
            key_rows.reshape(page_count, PAGE, local_width),
            value_rows.reshape(page_count, PAGE, local_width),
        ],
        axis=1,
    )
    kv_pages = jnp.take(both_blocks, inverse, axis=0)
    return (layer_out, kv_pages)


def solution(mesh):
    return jax.shard_map(
        local,
        mesh=mesh,
        in_specs=(
            P("grp", None),
            P(),
            P(None, None, "tp"),
            P("tp", None),
            P("grp", "tp", None),
            P("grp", None, None, "tp"),
            P("grp", "tp", None),
            P("grp", None, "tp"),
            P(),
            P(),
            P(),
            P("grp", None),
        ),
        out_specs=(P("grp", "tp"), P("grp", None, None, "tp")),
        check_vma=False,
    )
```
